128 devices in a mesh: grp: 4 (over y), slab: 32 (over z, x, core).
Axes of the slice: x: 4, y: 4, z: 4, core: 2. Of those that a mesh axis runs over, the one named last changes fastest.
Arguments:
- vessel_start: float32 [16384, 128], P(('grp', 'slab')), may hold values from -6 to 6
- drive: float32 [16384, 128], P(('grp', 'slab')), may hold values from -6 to 6
- junction_gain: float32 [16384], P(('grp', 'slab')), may hold values from 0.5 to 2
- parent: int32 [16384], P(('grp', 'slab')), may hold values from 0 to 16383, as said below
- inverse_blocks: bfloat16 [16384, 128, 128], P(('grp', 'slab')), as said below
- wall_perm: float32 [16384, 128], P(('grp', 'slab')), may hold values from 0.2 to 2
- outside: float32 [16384, 128], P(('grp', 'slab')), may hold values from -6 to 6
- owner: int32 [16384, 1], P(('grp', 'slab')), may hold values from 0 to 127; in each aligned block of 128 rows (0 to 127, 128 to 255, ...) at most 2 rows name the same one
- target: int32 [16384], P(('grp', 'slab')), may hold values from 0 to 4095
- kernel_id: int32 [16384], P(('grp', 'slab')), may hold values from 0 to 3
- kernels: bfloat16 [4, 128, 128], replicated, may hold values from -0.5 to 0.5
- tissue_start: float32 [512, 256, 512], P(('grp', 'slab')), may hold values from -6 to 6
- conduct: float32 [512, 256, 512], P(('grp', 'slab')), may hold values from 0.1 to 10
- base_source: float32 [512, 256, 512], P(('grp', 'slab')), may hold values from -6 to 6
Outputs:
- vessel_pressure: float32 [16384, 128], P(('grp', 'slab'))
- tissue_pressure: float32 [512, 256, 512], P(('grp', 'slab'))
The draws below stay inside these ranges and needn't reach their ends.
Inputs may be any that keep to these rules, and one draw needn't show every extreme that they name: Block 0's parent is the last block and the last block's parent is block 0. Within the blocks of one device no owner is named by more than 2 blocks. `inverse_blocks`: each block is the identity plus entries of order 0.05, except the first column below the diagonal, whose entries lie between 0.5 and 1.
All inputs are finite; a program needn't handle non-finite values.
Results may differ from the reference program's by a relative error of at most 0.0042.
Values sent between devices are 32-bit elements; how exact they have to be, the bound alone decides.
No kernel may reach another device: no remote copies, remote signals or barrier semaphores. Data moves between devices by JAX's collectives and lax.ppermute only.
A program may use at most 64 MiB of HBM per device.

```python
import math
import jax
import jax.numpy as jnp
import numpy as np
from jax import lax

NB = 128
XC = 256
YC = 512
SWEEPS = 3
NK = 4
CAP = 2
NBLK = 16384
ZN = 512
NCB = 4096
N_GRP = 4
N_SLAB = 32


def draw_inverse_blocks(key, part):
    spread_key, column_key = jax.random.split(key, 2)
    spread = 0.05 * jax.random.normal(spread_key, (NBLK, 128, 128), jnp.float32)
    column = jax.random.uniform(column_key, (NBLK, 128, 128), jnp.float32, 0.5, 1.0)
    rows = jnp.arange(128, dtype=jnp.int32)[:, None]
    cols = jnp.arange(128, dtype=jnp.int32)[None, :]
    first_column = ((cols == 0) & (rows >= 1))[None]
    spread = jnp.where(first_column, column, spread)
    return (spread + jnp.eye(128, dtype=jnp.float32)[None]).astype(jnp.bfloat16)


def draw_parent(key, part):
    first_key, second_key, third_key = jax.random.split(key, 3)
    home = jnp.arange(NBLK, dtype=jnp.int32) // NB
    local = home * NB + jax.random.randint(first_key, (NBLK,), 0, NB, jnp.int32)
    remote = jax.random.randint(second_key, (NBLK,), 0, NBLK, jnp.int32)
    coin = jax.random.randint(third_key, (NBLK,), 0, 2, jnp.int32)
    linked = jnp.where(coin == 0, local, remote)
    return linked.at[0].set(NBLK - 1).at[NBLK - 1].set(0)


def plant(entries, own_key, low, top_value):
    dims = entries.shape
    place = [jax.random.randint(jax.random.fold_in(own_key, axis), (), 0, dims[axis]) for axis in range(len(dims))]
    entries = entries.at[tuple(place)].set(low)
    longest = dims.index(max(dims))
    place[longest] = (place[longest] + 1) % dims[longest]
    return entries.at[tuple(place)].set(top_value)


def block_scale(rng, shape, cuts, low, largest):
    level = 1.0
    for position, parts in cuts:
        heights = jax.random.uniform(jax.random.fold_in(jax.random.fold_in(rng, 6), position), (parts,), jnp.float32, low / len(cuts), largest / len(cuts))
        level = level * jnp.repeat(jnp.exp(heights), shape[position] // parts).reshape((-1,) + (1,) * (len(shape) - 1 - position))
    return level


def assign_block(stream_key, own, number, rows, number_of, top, most, lean):
    sequence = jax.random.permutation(stream_key, number_of)
    heavy_load, common = load_shares(number_of, rows * top, most, lean, True), load_shares(number_of, rows * top, most, lean, False)
    places = jnp.arange(number_of)

    def named(lengths, turn):
        used = int((lengths > 0).sum())
        fixed = max(1, used // 4)
        passed = fixed + (places - fixed + turn * (used - fixed)) % max(1, number_of - fixed)
        return jnp.zeros((number_of,), jnp.int32).at[sequence[jnp.where(places < fixed, places, passed)]].set(jnp.asarray(lengths, jnp.int32))

    lengths = jnp.where(number % 4 == 0, named(heavy_load, number // 4), named(common, number - number // 4 - 1))
    mixed = jax.random.permutation(jax.random.fold_in(own, 3), number_of)
    source_of, sink = mixed[0:number_of // 2 * 2:2], mixed[1:number_of // 2 * 2:2]
    margin = jnp.minimum(lengths[source_of] - 1, most - lengths[sink]) // 2
    margin = jnp.where((source_of == sequence[0]) | (sink == sequence[0]) | (lengths[sink] == 0), 0, jnp.maximum(margin, 0))
    passed = jax.random.randint(jax.random.fold_in(own, 4), (number_of // 2,), 0, 1 << 20) % (margin + 1)
    lengths = lengths.at[source_of].add(-passed).at[sink].add(passed)
    labels = jnp.searchsorted(jnp.cumsum(lengths), jnp.arange(rows * top), side="right").astype(jnp.int32)
    listing = labels.reshape(top, rows).T
    listing = listing[jax.random.permutation(jax.random.fold_in(own, 1), rows)]
    turn = jax.random.randint(jax.random.fold_in(own, 2), (rows, 1), 0, top)
    return jnp.take_along_axis(listing, (jnp.arange(top)[None, :] + turn) % top, axis=1)


def load_shares(count, total, limit, slope, full):
    weights = [(1 << 20) // math.isqrt(grade ** slope) + 1 for grade in range(1, count + 1)]
    largest = limit if full else min(limit, max(-(-total // count), total * weights[0] // sum(weights)))
    least = 1 if total - largest >= count - 1 else 0
    given, surplus = [largest] + [least] * (count - 1), total - largest - least * (count - 1)
    while surplus > 0:
        candidates = [i for i in range(1, count) if given[i] < largest] or [i for i in range(1, count) if given[i] < limit]
        mass, left = sum([weights[i] for i in candidates]), surplus
        for i in candidates:
            extra = min(limit - given[i], max(1, left * weights[i] // mass), surplus)
            given[i] = given[i] + extra
            surplus = surplus - extra
    return np.array(given)


def noise(rng, shape, scale, most, pieces=(), held_as=jnp.bfloat16):
    drawn = scale * jax.random.normal(rng, shape, jnp.float32)
    if pieces:
        drawn = drawn * block_scale(rng, shape, pieces, -0.22, 0.18)
    return jnp.clip(drawn, -most, most).astype(held_as)


def setup_inputs(seed: int = 0) -> dict:
    keys = jax.random.split(jax.random.key(seed), 15)
    vessel_start = noise(keys[0], (NBLK, 128), 1.0, 6.0, ((0, 128),), jnp.float32)
    drive = noise(keys[1], (NBLK, 128), 1.0, 6.0, ((0, 128),), jnp.float32)
    junction_gain = jnp.clip(jnp.exp(math.log(2.0) - 1.3862944 * jax.random.uniform(keys[2], (NBLK,), jnp.float32) ** block_scale(keys[2], (NBLK,), ((0, 128),), -0.2, 0.2)), 0.5, 2.0)
    parent = draw_parent(jax.random.fold_in(keys[14], 71), 0)
    inverse_blocks = draw_inverse_blocks(jax.random.fold_in(keys[14], 71), 0)
    wall_perm = jnp.clip(jnp.exp(math.log(2.0) - 2.3025851 * jax.random.uniform(keys[5], (NBLK, 128), jnp.float32) ** block_scale(keys[5], (NBLK, 128), ((0, 128),), -0.2, 0.2)), 0.2, 2.0)
    outside = noise(keys[6], (NBLK, 128), 1.0, 6.0, ((0, 128),), jnp.float32)
    owner_keys = jax.random.split(jax.random.fold_in(keys[7], 1), NBLK // NB)
    owner_turns = jax.random.permutation(jax.random.fold_in(keys[7], 3), NBLK // NB)
    owner = jax.vmap(lambda own, number: assign_block(jax.random.fold_in(keys[7], 2), own, number, NB, N_GRP * N_SLAB, 1, CAP, 2))(owner_keys, owner_turns).reshape((NBLK, 1))
    target = plant(jax.random.randint(keys[8], (NBLK,), 0, NCB), jax.random.fold_in(keys[8], 1), 0, NCB - 1).astype(jnp.int32)
    kernel_id = plant(jax.random.randint(keys[9], (NBLK,), 0, NK), jax.random.fold_in(keys[9], 1), 0, NK - 1).astype(jnp.int32)
    kernels = noise(keys[10], (NK, 128, 128), 128 ** -0.5, 0.5)
    tissue_start = noise(keys[11], (ZN, XC, YC), 1.0, 6.0, ((0, 128),), jnp.float32)
    conduct = jnp.clip(jnp.exp(math.log(10.0) - 4.6051702 * jax.random.uniform(keys[12], (ZN, XC, YC), jnp.float32) ** block_scale(keys[12], (ZN, XC, YC), ((0, 128),), -0.2, 0.2)), 0.1, 10.0)
    base_source = noise(keys[13], (ZN, XC, YC), 1.0, 6.0, ((0, 128),), jnp.float32)
    return dict(vessel_start=vessel_start, drive=drive, junction_gain=junction_gain, parent=parent, inverse_blocks=inverse_blocks, wall_perm=wall_perm, outside=outside, owner=owner, target=target, kernel_id=kernel_id, kernels=kernels, tissue_start=tissue_start, conduct=conduct, base_source=base_source)


UPTAKE = 0.5


def neighbours(values):
    return [values[2:, 1:-1, 1:-1], values[:-2, 1:-1, 1:-1], values[1:-1, 2:, 1:-1], values[1:-1, :-2, 1:-1], values[1:-1, 1:-1, 2:], values[1:-1, 1:-1, :-2]]


def relax(padded_p, padded_k, source):
    centre = padded_k[1:-1, 1:-1, 1:-1]
    numerator = source
    denominator = jnp.full(centre.shape, UPTAKE, jnp.float32)
    for p_side, k_side in zip(neighbours(padded_p), neighbours(padded_k)):
        facing = 0.5 * (centre + k_side)
        numerator = numerator + facing * p_side
        denominator = denominator + facing
    return numerator / denominator


def tissue_sweep(pressure, conduct, source):
    padded_p = jnp.pad(pressure, 1)
    padded_k = jnp.pad(conduct, 1)

    def one_plane(plane):
        return relax(lax.dynamic_slice_in_dim(padded_p, plane, 3, 0), lax.dynamic_slice_in_dim(padded_k, plane, 3, 0), lax.dynamic_slice_in_dim(source, plane, 1, 0))

    planes = lax.map(one_plane, jnp.arange(pressure.shape[0], dtype=jnp.int32))
    return planes.reshape(pressure.shape)


def apply_inverse(operands):
    return jnp.einsum("bij,bj->bi", operands[0].astype(jnp.float32), operands[1].astype(jnp.float32))


def reference(vessel_start, drive, junction_gain, parent, inverse_blocks, wall_perm, outside, owner, target, kernel_id, kernels, tissue_start, conduct, base_source):
    pressure = vessel_start
    blocks = inverse_blocks.reshape(-1, NB, 128, 128)
    for sweep_index in range(SWEEPS):
        exit_values = pressure[:, -1]
        inflow = exit_values[parent]
        right_side = drive.at[:, 0].add(junction_gain * inflow).astype(jnp.bfloat16)
        pressure = lax.map(apply_inverse, (blocks, right_side.reshape(-1, NB, 128))).reshape(pressure.shape)
    leak = (wall_perm * (pressure - outside)).astype(jnp.bfloat16)
    spread = jnp.einsum("bs,ksc->kbc", leak.astype(jnp.float32), kernels.astype(jnp.float32))
    picks = kernel_id[None, :] == jnp.arange(NK, dtype=jnp.int32)[:, None]
    cells = jnp.sum(jnp.where(picks[:, :, None], spread, 0.0), axis=0)
    total_blocks = conduct.shape[0] * conduct.shape[1] * conduct.shape[2] // 128
    slab_blocks = total_blocks // (N_GRP * N_SLAB)
    where_to = (owner[:, 0] * slab_blocks + target).astype(jnp.int32)
    leakage = jax.ops.segment_sum(cells, where_to, num_segments=total_blocks)
    source = base_source + leakage.reshape(conduct.shape)
    tissue = tissue_sweep(tissue_start, conduct, source)
    tissue = tissue_sweep(tissue, conduct, source)
    return pressure, tissue
```

```python
import jax
import jax.numpy as jnp
from jax import lax
from jax.sharding import PartitionSpec as P

UPTAKE = 0.5
AXES = ("grp", "slab")


def padded(cells, sides, width):
    for axis, dim in sides:
        count = lax.axis_size(axis)
        ends = count - 1
        head = lax.slice_in_dim(cells, 0, width, axis=dim)
        tail = lax.slice_in_dim(cells, cells.shape[dim] - width, cells.shape[dim], axis=dim)
        cells = jnp.concatenate(
            [
                lax.ppermute(tail, axis, [(i, (i + 1) % count) for i in range(ends)]),
                cells,
                lax.ppermute(head, axis, [((i + 1) % count, i) for i in range(ends)]),
            ],
            axis=dim,
        )
    return cells


def neighbours(values):
    return [
        values[2:, 1:-1, 1:-1],
        values[:-2, 1:-1, 1:-1],
        values[1:-1, 2:, 1:-1],
        values[1:-1, :-2, 1:-1],
        values[1:-1, 1:-1, 2:],
        values[1:-1, 1:-1, :-2],
    ]


def relax(padded_p, padded_k, source):
    centre = padded_k[1:-1, 1:-1, 1:-1]
    numerator = source
    denominator = jnp.full(centre.shape, UPTAKE, jnp.float32)
    for p_side, k_side in zip(neighbours(padded_p), neighbours(padded_k)):
        facing = 0.5 * (centre + k_side)
        numerator = numerator + facing * p_side
        denominator = denominator + facing
    return numerator / denominator


def pad_sides(values):
    return jnp.pad(values, ((0, 0), (1, 1), (1, 1)))


def bf16_round(x):
    return x.astype(jnp.bfloat16).astype(jnp.float32)


def on_device(
    vessel_start,
    drive,
    junction_gain,
    parent,
    inverse_blocks,
    wall_perm,
    outside,
    owner,
    target,
    kernel_id,
    kernels,
    tissue_start,
    conduct,
    base_source,
):
    devices = lax.axis_size(AXES)
    nb = drive.shape[0]
    seg = drive.shape[1]
    lane = jnp.arange(seg, dtype=jnp.int32)[None, :]
    fixed_rhs = jnp.where(lane == 0, 0.0, drive).astype(jnp.bfloat16)
    base = jnp.einsum(
        "bij,bj->bi", inverse_blocks, fixed_rhs, preferred_element_type=jnp.float32
    )
    first_col = inverse_blocks[:, :, 0].astype(jnp.float32)
    exit_base = base[:, -1]
    exit_col = first_col[:, -1]
    drive0 = drive[:, 0]
    packed = jnp.stack(
        [
            exit_base,
            exit_col,
            drive0,
            junction_gain,
            vessel_start[:, -1],
            parent.astype(jnp.float32),
        ]
    ).reshape(1, 6 * nb)
    sent = jnp.broadcast_to(packed, (devices, 6 * nb))
    got = lax.all_to_all(sent, AXES, 0, 0, tiled=True)
    table = got.reshape(devices, 6, nb).transpose(1, 0, 2).reshape(6, devices * nb)
    all_parent = table[5].astype(jnp.int32)
    p1 = parent
    p2 = all_parent[p1]
    p3 = all_parent[p2]
    at2 = table[:, p2]
    at1 = table[:, p1]
    x0 = table[4][p3]
    exit1 = at2[0] + at2[1] * bf16_round(at2[2] + at2[3] * x0)
    exit2 = at1[0] + at1[1] * bf16_round(at1[2] + at1[3] * exit1)
    r0 = bf16_round(drive0 + junction_gain * exit2)
    pressure = base + first_col * r0[:, None]
    leak = (wall_perm * (pressure - outside)).astype(jnp.bfloat16)
    destination = owner[:, 0]
    same = destination[:, None] == destination[None, :]
    earlier = jnp.arange(nb)[None, :] < jnp.arange(nb)[:, None]
    slot = jnp.sum((same & earlier).astype(jnp.int32), axis=1)
    capacity = 2
    row_of = destination * capacity + slot
    slots = devices * capacity
    onehot = row_of[None, :] == jnp.arange(slots, dtype=jnp.int32)[:, None]
    leak_sent = jnp.dot(
        onehot.astype(jnp.bfloat16), leak, preferred_element_type=jnp.float32
    ).astype(jnp.bfloat16)
    kid_sent = jnp.sum(jnp.where(onehot, kernel_id[None, :], 0), axis=1)
    tgt_sent = jnp.sum(jnp.where(onehot, target[None, :], 0), axis=1)
    cells = jnp.zeros((slots, seg), jnp.float32)
    for k in range(kernels.shape[0]):
        part = jnp.dot(leak_sent, kernels[k], preferred_element_type=jnp.float32)
        cells = jnp.where((kid_sent == k)[:, None], part, cells)
    tgt_row = jnp.pad(
        tgt_sent.astype(jnp.float32).reshape(devices, capacity), ((0, 0), (0, seg - capacity))
    )
    send = jnp.concatenate(
        [cells.reshape(devices, capacity, seg), tgt_row[:, None, :]], axis=1
    )
    recv = lax.all_to_all(send, AXES, 0, 0, tiled=True)
    got_rows = recv[:, :capacity, :].reshape(slots, seg)
    got_index = recv[:, capacity, :capacity].reshape(slots).astype(jnp.int32)
    cell_blocks = tissue_start.size // seg
    leakage = jax.ops.segment_sum(got_rows, got_index, num_segments=cell_blocks)
    source = base_source + leakage.reshape(base_source.shape)
    stacked = jnp.stack([tissue_start, conduct])
    wide = padded(stacked, ((AXES, 1),), 1)
    padded_k = pad_sides(wide[1])
    first = relax(pad_sides(wide[0]), padded_k, source)
    second = padded(first, ((AXES, 0),), 1)
    tissue = relax(pad_sides(second), padded_k, source)
    return (pressure, tissue)


def solution(mesh):
    in_specs = (
        P(AXES, None),
        P(AXES, None),
        P(AXES),
        P(AXES),
        P(AXES, None, None),
        P(AXES, None),
        P(AXES, None),
        P(AXES, None),
        P(AXES),
        P(AXES),
        P(),
        P(AXES, None, None),
        P(AXES, None, None),
        P(AXES, None, None),
    )
    out_specs = (P(AXES, None), P(AXES, None, None))
    return jax.shard_map(
        on_device, mesh=mesh, in_specs=in_specs, out_specs=out_specs, check_vma=False
    )
```

```python
import jax
import jax.numpy as jnp
from jax import lax
from jax.sharding import PartitionSpec as P

UPTAKE = 0.5
AXES = ("grp", "slab")


def padded(cells, sides, width):
    for axis, dim in sides:
        count = lax.axis_size(axis)
        ends = count - 1
        head = lax.slice_in_dim(cells, 0, width, axis=dim)
        tail = lax.slice_in_dim(cells, cells.shape[dim] - width, cells.shape[dim], axis=dim)
        cells = jnp.concatenate(
            [
                lax.ppermute(tail, axis, [(i, (i + 1) % count) for i in range(ends)]),
                cells,
                lax.ppermute(head, axis, [((i + 1) % count, i) for i in range(ends)]),
            ],
            axis=dim,
        )
    return cells


def neighbours(values):
    return [
        values[2:, 1:-1, 1:-1],
        values[:-2, 1:-1, 1:-1],
        values[1:-1, 2:, 1:-1],
        values[1:-1, :-2, 1:-1],
        values[1:-1, 1:-1, 2:],
        values[1:-1, 1:-1, :-2],
    ]


def relax(padded_p, padded_k, source):
    centre = padded_k[1:-1, 1:-1, 1:-1]
    numerator = source
    denominator = jnp.full(centre.shape, UPTAKE, jnp.float32)
    for p_side, k_side in zip(neighbours(padded_p), neighbours(padded_k)):
        facing = 0.5 * (centre + k_side)
        numerator = numerator + facing * p_side
        denominator = denominator + facing
    return numerator / denominator


def relax_parts(padded_p, padded_k, source):
    centre = padded_k[1:-1, 1:-1, 1:-1]
    numerator = source
    denominator = jnp.full(centre.shape, UPTAKE, jnp.float32)
    for p_side, k_side in zip(neighbours(padded_p), neighbours(padded_k)):
        facing = 0.5 * (centre + k_side)
        numerator = numerator + facing * p_side
        denominator = denominator + facing
    return numerator, denominator


def pad_sides(values):
    return jnp.pad(values, ((0, 0), (1, 1), (1, 1)))


def bf16_round(x):
    return x.astype(jnp.bfloat16).astype(jnp.float32)


def on_device(
    vessel_start,
    drive,
    junction_gain,
    parent,
    inverse_blocks,
    wall_perm,
    outside,
    owner,
    target,
    kernel_id,
    kernels,
    tissue_start,
    conduct,
    base_source,
):
    devices = lax.axis_size(AXES)
    nb = drive.shape[0]
    seg = drive.shape[1]
    lane = jnp.arange(seg, dtype=jnp.int32)[None, :]
    fixed_rhs = jnp.where(lane == 0, 0.0, drive).astype(jnp.bfloat16)
    base = jnp.einsum(
        "bij,bj->bi", inverse_blocks, fixed_rhs, preferred_element_type=jnp.float32
    )
    first_col = inverse_blocks[:, :, 0].astype(jnp.float32)
    exit_base = base[:, -1]
    exit_col = first_col[:, -1]
    drive0 = drive[:, 0]
    packed = jnp.stack(
        [
            exit_base,
            exit_col,
            drive0,
            junction_gain,
            vessel_start[:, -1],
            parent.astype(jnp.float32),
        ]
    ).reshape(1, 6 * nb)
    sent = jnp.broadcast_to(packed, (devices, 6 * nb))
    got = lax.all_to_all(sent, AXES, 0, 0, tiled=True).reshape(-1)
    fields = jnp.arange(6, dtype=jnp.int32)[:, None] * nb

    def fetch(index):
        flat = (index // nb) * (6 * nb) + index % nb
        return got[flat[None, :] + fields]

    at1 = fetch(parent)
    p2 = at1[5].astype(jnp.int32)
    at2 = fetch(p2)
    p3 = at2[5].astype(jnp.int32)
    x0 = got[(p3 // nb) * (6 * nb) + 4 * nb + p3 % nb]
    exit1 = at2[0] + at2[1] * bf16_round(at2[2] + at2[3] * x0)
    exit2 = at1[0] + at1[1] * bf16_round(at1[2] + at1[3] * exit1)
    r0 = bf16_round(drive0 + junction_gain * exit2)
    pressure = base + first_col * r0[:, None]
    leak = (wall_perm * (pressure - outside)).astype(jnp.bfloat16)
    destination = owner[:, 0]
    same = destination[:, None] == destination[None, :]
    earlier = jnp.arange(nb)[None, :] < jnp.arange(nb)[:, None]
    slot = jnp.sum((same & earlier).astype(jnp.int32), axis=1)
    capacity = 2
    row_of = destination * capacity + slot
    slots = devices * capacity
    onehot = row_of[None, :] == jnp.arange(slots, dtype=jnp.int32)[:, None]
    leak_sent = jnp.dot(
        onehot.astype(jnp.bfloat16), leak, preferred_element_type=jnp.float32
    ).astype(jnp.bfloat16)
    kid_sent = jnp.sum(jnp.where(onehot, kernel_id[None, :], 0), axis=1)
    tgt_sent = jnp.sum(jnp.where(onehot, target[None, :], 0), axis=1)
    cells = jnp.zeros((slots, seg), jnp.float32)
    for k in range(kernels.shape[0]):
        part = jnp.dot(leak_sent, kernels[k], preferred_element_type=jnp.float32)
        cells = jnp.where((kid_sent == k)[:, None], part, cells)
    tgt_row = jnp.pad(
        tgt_sent.astype(jnp.float32).reshape(devices, capacity), ((0, 0), (0, seg - capacity))
    )
    send = jnp.concatenate(
        [cells.reshape(devices, capacity, seg), tgt_row[:, None, :]], axis=1
    )
    recv = lax.all_to_all(
        send.reshape(devices, (capacity + 1) * seg), AXES, 0, 0, tiled=True
    ).reshape(devices, capacity + 1, seg)
    got_rows = recv[:, :capacity, :].reshape(slots, seg)
    got_index = recv[:, capacity, :capacity].reshape(slots).astype(jnp.int32)
    cell_blocks = tissue_start.size // seg
    leakage = jax.ops.segment_sum(got_rows, got_index, num_segments=cell_blocks)
    leak_field = leakage.reshape(base_source.shape)
    source = base_source + leak_field
    stacked = jnp.stack([tissue_start, conduct])
    wide = padded(stacked, ((AXES, 1),), 1)
    padded_k = pad_sides(wide[1])
    partial, denominator = relax_parts(pad_sides(wide[0]), padded_k, base_source)
    first = (partial + leak_field) / denominator
    second = padded(first, ((AXES, 0),), 1)
    tissue = relax(pad_sides(second), padded_k, source)
    return (pressure, tissue)


def solution(mesh):
    in_specs = (
        P(AXES, None),
        P(AXES, None),
        P(AXES),
        P(AXES),
        P(AXES, None, None),
        P(AXES, None),
        P(AXES, None),
        P(AXES, None),
        P(AXES),
        P(AXES),
        P(),
        P(AXES, None, None),
        P(AXES, None, None),
        P(AXES, None, None),
    )
    out_specs = (P(AXES, None), P(AXES, None, None))
    return jax.shard_map(
        on_device, mesh=mesh, in_specs=in_specs, out_specs=out_specs, check_vma=False
    )
```

```python
import jax
import jax.numpy as jnp
from jax import lax
from jax.sharding import PartitionSpec as P

UPTAKE = 0.5
AXES = ("grp", "slab")


def padded(cells, sides, width):
    for axis, dim in sides:
        count = lax.axis_size(axis)
        ends = count - 1
        head = lax.slice_in_dim(cells, 0, width, axis=dim)
        tail = lax.slice_in_dim(cells, cells.shape[dim] - width, cells.shape[dim], axis=dim)
        cells = jnp.concatenate(
            [
                lax.ppermute(tail, axis, [(i, (i + 1) % count) for i in range(ends)]),
                cells,
                lax.ppermute(head, axis, [((i + 1) % count, i) for i in range(ends)]),
            ],
            axis=dim,
        )
    return cells


def neighbours(values):
    return [
        values[2:, 1:-1, 1:-1],
        values[:-2, 1:-1, 1:-1],
        values[1:-1, 2:, 1:-1],
        values[1:-1, :-2, 1:-1],
        values[1:-1, 1:-1, 2:],
        values[1:-1, 1:-1, :-2],
    ]


def relax(padded_p, padded_k, source):
    centre = padded_k[1:-1, 1:-1, 1:-1]
    numerator = source
    denominator = jnp.full(centre.shape, UPTAKE, jnp.float32)
    for p_side, k_side in zip(neighbours(padded_p), neighbours(padded_k)):
        facing = 0.5 * (centre + k_side)
        numerator = numerator + facing * p_side
        denominator = denominator + facing
    return numerator / denominator


def relax_parts(padded_p, padded_k, source):
    centre = padded_k[1:-1, 1:-1, 1:-1]
    numerator = source
    denominator = jnp.full(centre.shape, UPTAKE, jnp.float32)
    for p_side, k_side in zip(neighbours(padded_p), neighbours(padded_k)):
        facing = 0.5 * (centre + k_side)
        numerator = numerator + facing * p_side
        denominator = denominator + facing
    return numerator, denominator


def pad_sides(values):
    return jnp.pad(values, ((0, 0), (1, 1), (1, 1)))


def bf16_round(x):
    return x.astype(jnp.bfloat16).astype(jnp.float32)


def on_device(
    vessel_start,
    drive,
    junction_gain,
    parent,
    inverse_blocks,
    wall_perm,
    outside,
    owner,
    target,
    kernel_id,
    kernels,
    tissue_start,
    conduct,
    base_source,
):
    devices = lax.axis_size(AXES)
    nb = drive.shape[0]
    seg = drive.shape[1]
    lane = jnp.arange(seg, dtype=jnp.int32)[None, :]
    fixed_rhs = jnp.where(lane == 0, 0.0, drive).astype(jnp.bfloat16)
    unit = jnp.broadcast_to((lane == 0).astype(jnp.bfloat16), (nb, seg))
    both = jnp.einsum(
        "bij,cbj->cbi",
        inverse_blocks,
        jnp.stack([fixed_rhs, unit]),
        preferred_element_type=jnp.float32,
    )
    base = both[0]
    first_col = both[1]
    exit_base = base[:, -1]
    exit_col = first_col[:, -1]
    drive0 = drive[:, 0]
    packed = jnp.stack(
        [
            exit_base,
            exit_col,
            drive0,
            junction_gain,
            vessel_start[:, -1],
            parent.astype(jnp.float32),
        ]
    ).reshape(1, 6 * nb)
    sent = jnp.broadcast_to(packed, (devices, 6 * nb))
    got = lax.all_to_all(sent, AXES, 0, 0, tiled=True)
    owners = jnp.arange(devices, dtype=jnp.int32)[None, :]
    within = jnp.arange(nb, dtype=jnp.int32)[None, :]

    def fetch(index):
        pick = (index // nb)[:, None] == owners
        rows = jnp.dot(
            pick.astype(jnp.float32), got, precision=lax.Precision.HIGHEST
        ).reshape(index.shape[0], 6, nb)
        lanes = ((index % nb)[:, None] == within)[:, None, :]
        return jnp.sum(jnp.where(lanes, rows, 0.0), axis=2).T

    at1 = fetch(parent)
    p2 = jnp.round(at1[5]).astype(jnp.int32)
    at2 = fetch(p2)
    p3 = jnp.round(at2[5]).astype(jnp.int32)
    x0 = fetch(p3)[4]
    exit1 = at2[0] + at2[1] * bf16_round(at2[2] + at2[3] * x0)
    exit2 = at1[0] + at1[1] * bf16_round(at1[2] + at1[3] * exit1)
    r0 = bf16_round(drive0 + junction_gain * exit2)
    pressure = base + first_col * r0[:, None]
    leak = (wall_perm * (pressure - outside)).astype(jnp.bfloat16)
    destination = owner[:, 0]
    same = destination[:, None] == destination[None, :]
    earlier = jnp.arange(nb)[None, :] < jnp.arange(nb)[:, None]
    slot = jnp.sum((same & earlier).astype(jnp.int32), axis=1)
    capacity = 2
    row_of = destination * capacity + slot
    slots = devices * capacity
    onehot = row_of[None, :] == jnp.arange(slots, dtype=jnp.int32)[:, None]
    leak_sent = jnp.dot(
        onehot.astype(jnp.bfloat16), leak, preferred_element_type=jnp.float32
    ).astype(jnp.bfloat16)
    kid_sent = jnp.sum(jnp.where(onehot, kernel_id[None, :], 0), axis=1)
    tgt_sent = jnp.sum(jnp.where(onehot, target[None, :], 0), axis=1)
    cells = jnp.zeros((slots, seg), jnp.float32)
    for k in range(kernels.shape[0]):
        part = jnp.dot(leak_sent, kernels[k], preferred_element_type=jnp.float32)
        cells = jnp.where((kid_sent == k)[:, None], part, cells)
    tgt_row = jnp.pad(
        tgt_sent.astype(jnp.float32).reshape(devices, capacity), ((0, 0), (0, seg - capacity))
    )
    send = jnp.concatenate(
        [cells.reshape(devices, capacity, seg), tgt_row[:, None, :]], axis=1
    )
    recv = lax.all_to_all(
        send.reshape(devices, (capacity + 1) * seg), AXES, 0, 0, tiled=True
    ).reshape(devices, capacity + 1, seg)
    got_rows = recv[:, :capacity, :].reshape(slots, seg)
    got_index = recv[:, capacity, :capacity].reshape(slots).astype(jnp.int32)
    cell_blocks = tissue_start.size // seg
    leakage = jax.ops.segment_sum(got_rows, got_index, num_segments=cell_blocks)
    leak_field = leakage.reshape(base_source.shape)
    source = base_source + leak_field
    stacked = jnp.stack([tissue_start, conduct])
    wide = padded(stacked, ((AXES, 1),), 1)
    padded_k = pad_sides(wide[1])
    partial, denominator = relax_parts(pad_sides(wide[0]), padded_k, base_source)
    first = (partial + leak_field) / denominator
    second = padded(first, ((AXES, 0),), 1)
    tissue = relax(pad_sides(second), padded_k, source)
    return (pressure, tissue)


def solution(mesh):
    in_specs = (
        P(AXES, None),
        P(AXES, None),
        P(AXES),
        P(AXES),
        P(AXES, None, None),
        P(AXES, None),
        P(AXES, None),
        P(AXES, None),
        P(AXES),
        P(AXES),
        P(),
        P(AXES, None, None),
        P(AXES, None, None),
        P(AXES, None, None),
    )
    out_specs = (P(AXES, None), P(AXES, None, None))
    return jax.shard_map(
        on_device, mesh=mesh, in_specs=in_specs, out_specs=out_specs, check_vma=False
    )
```

```python
import jax
import jax.numpy as jnp
from jax import lax
from jax.sharding import PartitionSpec as P

UPTAKE = 0.5
AXES = ("grp", "slab")


def padded(cells, sides, width):
    for axis, dim in sides:
        count = lax.axis_size(axis)
        ends = count - 1
        head = lax.slice_in_dim(cells, 0, width, axis=dim)
        tail = lax.slice_in_dim(cells, cells.shape[dim] - width, cells.shape[dim], axis=dim)
        cells = jnp.concatenate(
            [
                lax.ppermute(tail, axis, [(i, (i + 1) % count) for i in range(ends)]),
                cells,
                lax.ppermute(head, axis, [((i + 1) % count, i) for i in range(ends)]),
            ],
            axis=dim,
        )
    return cells


def neighbours(values):
    return [
        values[2:, 1:-1, 1:-1],
        values[:-2, 1:-1, 1:-1],
        values[1:-1, 2:, 1:-1],
        values[1:-1, :-2, 1:-1],
        values[1:-1, 1:-1, 2:],
        values[1:-1, 1:-1, :-2],
    ]


def relax(padded_p, padded_k, source):
    centre = padded_k[1:-1, 1:-1, 1:-1]
    numerator = source
    denominator = jnp.full(centre.shape, UPTAKE, jnp.float32)
    for p_side, k_side in zip(neighbours(padded_p), neighbours(padded_k)):
        facing = 0.5 * (centre + k_side)
        numerator = numerator + facing * p_side
        denominator = denominator + facing
    return numerator / denominator


def relax_parts(padded_p, padded_k, source):
    centre = padded_k[1:-1, 1:-1, 1:-1]
    numerator = source
    denominator = jnp.full(centre.shape, UPTAKE, jnp.float32)
    for p_side, k_side in zip(neighbours(padded_p), neighbours(padded_k)):
        facing = 0.5 * (centre + k_side)
        numerator = numerator + facing * p_side
        denominator = denominator + facing
    return numerator, denominator


def pad_sides(values):
    return jnp.pad(values, ((0, 0), (1, 1), (1, 1)))


def bf16_round(x):
    return x.astype(jnp.bfloat16).astype(jnp.float32)


def on_device(
    vessel_start,
    drive,
    junction_gain,
    parent,
    inverse_blocks,
    wall_perm,
    outside,
    owner,
    target,
    kernel_id,
    kernels,
    tissue_start,
    conduct,
    base_source,
):
    devices = lax.axis_size(AXES)
    nb = drive.shape[0]
    seg = drive.shape[1]
    lane = jnp.arange(seg, dtype=jnp.int32)[None, :]
    fixed_rhs = jnp.where(lane == 0, 0.0, drive).astype(jnp.bfloat16)
    unit = jnp.broadcast_to((lane == 0).astype(jnp.bfloat16), (nb, seg))
    both = jnp.einsum(
        "bij,cbj->cbi",
        inverse_blocks,
        jnp.stack([fixed_rhs, unit]),
        preferred_element_type=jnp.float32,
    )
    base = both[0]
    first_col = both[1]
    last_row = inverse_blocks[:, -1, :].astype(jnp.float32)
    exit_base = jnp.sum(last_row * fixed_rhs.astype(jnp.float32), axis=1)
    exit_col = last_row[:, 0]
    drive0 = drive[:, 0]
    packed = jnp.stack(
        [
            exit_base,
            exit_col,
            drive0,
            junction_gain,
            vessel_start[:, -1],
            parent.astype(jnp.float32),
        ]
    ).reshape(1, 6 * nb)
    sent = jnp.broadcast_to(packed, (devices, 6 * nb))
    got = lax.all_to_all(sent, AXES, 0, 0, tiled=True)
    owners = jnp.arange(devices, dtype=jnp.int32)[None, :]
    within = jnp.arange(nb, dtype=jnp.int32)[None, :]

    def fetch(index):
        pick = (index // nb)[:, None] == owners
        rows = jnp.dot(
            pick.astype(jnp.float32), got, precision=lax.Precision.HIGHEST
        ).reshape(index.shape[0], 6, nb)
        lanes = ((index % nb)[:, None] == within)[:, None, :]
        return jnp.sum(jnp.where(lanes, rows, 0.0), axis=2).T

    at1 = fetch(parent)
    p2 = jnp.round(at1[5]).astype(jnp.int32)
    at2 = fetch(p2)
    p3 = jnp.round(at2[5]).astype(jnp.int32)
    x0 = fetch(p3)[4]
    exit1 = at2[0] + at2[1] * bf16_round(at2[2] + at2[3] * x0)
    exit2 = at1[0] + at1[1] * bf16_round(at1[2] + at1[3] * exit1)
    r0 = bf16_round(drive0 + junction_gain * exit2)
    pressure = base + first_col * r0[:, None]
    leak = (wall_perm * (pressure - outside)).astype(jnp.bfloat16)
    destination = owner[:, 0]
    same = destination[:, None] == destination[None, :]
    earlier = jnp.arange(nb)[None, :] < jnp.arange(nb)[:, None]
    slot = jnp.sum((same & earlier).astype(jnp.int32), axis=1)
    capacity = 2
    row_of = destination * capacity + slot
    slots = devices * capacity
    onehot = row_of[None, :] == jnp.arange(slots, dtype=jnp.int32)[:, None]
    leak_sent = jnp.dot(
        onehot.astype(jnp.bfloat16), leak, preferred_element_type=jnp.float32
    ).astype(jnp.bfloat16)
    kid_sent = jnp.sum(jnp.where(onehot, kernel_id[None, :], 0), axis=1)
    tgt_sent = jnp.sum(jnp.where(onehot, target[None, :], 0), axis=1)
    cells = jnp.zeros((slots, seg), jnp.float32)
    for k in range(kernels.shape[0]):
        part = jnp.dot(leak_sent, kernels[k], preferred_element_type=jnp.float32)
        cells = jnp.where((kid_sent == k)[:, None], part, cells)
    tgt_row = jnp.pad(
        tgt_sent.astype(jnp.float32).reshape(devices, capacity), ((0, 0), (0, seg - capacity))
    )
    send = jnp.concatenate(
        [cells.reshape(devices, capacity, seg), tgt_row[:, None, :]], axis=1
    )
    recv = lax.all_to_all(
        send.reshape(devices, (capacity + 1) * seg), AXES, 0, 0, tiled=True
    ).reshape(devices, capacity + 1, seg)
    got_rows = recv[:, :capacity, :].reshape(slots, seg)
    got_index = recv[:, capacity, :capacity].reshape(slots).astype(jnp.int32)
    cell_blocks = tissue_start.size // seg
    leakage = jax.ops.segment_sum(got_rows, got_index, num_segments=cell_blocks)
    leak_field = leakage.reshape(base_source.shape)
    source = base_source + leak_field
    stacked = jnp.stack([tissue_start, conduct])
    wide = padded(stacked, ((AXES, 1),), 1)
    padded_k = pad_sides(wide[1])
    partial, denominator = relax_parts(pad_sides(wide[0]), padded_k, base_source)
    first = (partial + leak_field) / denominator
    second = padded(first, ((AXES, 0),), 1)
    tissue = relax(pad_sides(second), padded_k, source)
    return (pressure, tissue)


def solution(mesh):
    in_specs = (
        P(AXES, None),
        P(AXES, None),
        P(AXES),
        P(AXES),
        P(AXES, None, None),
        P(AXES, None),
        P(AXES, None),
        P(AXES, None),
        P(AXES),
        P(AXES),
        P(),
        P(AXES, None, None),
        P(AXES, None, None),
        P(AXES, None, None),
    )
    out_specs = (P(AXES, None), P(AXES, None, None))
    return jax.shard_map(
        on_device, mesh=mesh, in_specs=in_specs, out_specs=out_specs, check_vma=False
    )
```

```python
import jax
import jax.numpy as jnp
from jax import lax
from jax.sharding import PartitionSpec as P

UPTAKE = 0.5
AXES = ("grp", "slab")


def padded(cells, sides, width):
    for axis, dim in sides:
        count = lax.axis_size(axis)
        ends = count - 1
        head = lax.slice_in_dim(cells, 0, width, axis=dim)
        tail = lax.slice_in_dim(cells, cells.shape[dim] - width, cells.shape[dim], axis=dim)
        cells = jnp.concatenate(
            [
                lax.ppermute(tail, axis, [(i, (i + 1) % count) for i in range(ends)]),
                cells,
                lax.ppermute(head, axis, [((i + 1) % count, i) for i in range(ends)]),
            ],
            axis=dim,
        )
    return cells


def neighbours(values):
    return [
        values[2:, 1:-1, 1:-1],
        values[:-2, 1:-1, 1:-1],
        values[1:-1, 2:, 1:-1],
        values[1:-1, :-2, 1:-1],
        values[1:-1, 1:-1, 2:],
        values[1:-1, 1:-1, :-2],
    ]


def relax(padded_p, padded_k, source):
    centre = padded_k[1:-1, 1:-1, 1:-1]
    numerator = source
    denominator = jnp.full(centre.shape, UPTAKE, jnp.float32)
    for p_side, k_side in zip(neighbours(padded_p), neighbours(padded_k)):
        facing = 0.5 * (centre + k_side)
        numerator = numerator + facing * p_side
        denominator = denominator + facing
    return numerator / denominator


def relax_parts(padded_p, padded_k, source):
    centre = padded_k[1:-1, 1:-1, 1:-1]
    numerator = source
    denominator = jnp.full(centre.shape, UPTAKE, jnp.float32)
    for p_side, k_side in zip(neighbours(padded_p), neighbours(padded_k)):
        facing = 0.5 * (centre + k_side)
        numerator = numerator + facing * p_side
        denominator = denominator + facing
    return numerator, denominator


def pad_sides(values):
    return jnp.pad(values, ((0, 0), (1, 1), (1, 1)))


def bf16_round(x):
    return x.astype(jnp.bfloat16).astype(jnp.float32)


def on_device_body(
    vessel_start,
    drive,
    junction_gain,
    parent,
    inverse_blocks,
    wall_perm,
    outside,
    owner,
    target,
    kernel_id,
    kernels,
    tissue_start,
    conduct,
    base_source,
):
    devices = lax.axis_size(AXES)
    nb = drive.shape[0]
    seg = drive.shape[1]
    lane = jnp.arange(seg, dtype=jnp.int32)[None, :]
    fixed_rhs = jnp.where(lane == 0, 0.0, drive).astype(jnp.bfloat16)
    unit = jnp.broadcast_to((lane == 0).astype(jnp.bfloat16), (nb, seg))
    both = jnp.einsum(
        "bij,cbj->cbi",
        inverse_blocks,
        jnp.stack([fixed_rhs, unit]),
        preferred_element_type=jnp.float32,
    )
    base = both[0]
    first_col = both[1]
    last_row = inverse_blocks[:, -1, :].astype(jnp.float32)
    exit_base = jnp.sum(last_row * fixed_rhs.astype(jnp.float32), axis=1)
    exit_col = last_row[:, 0]
    drive0 = drive[:, 0]
    packed = jnp.stack(
        [
            exit_base,
            exit_col,
            drive0,
            junction_gain,
            vessel_start[:, -1],
            parent.astype(jnp.float32),
        ]
    ).reshape(1, 6 * nb)
    sent = jnp.broadcast_to(packed, (devices, 6 * nb))
    got = lax.all_to_all(sent, AXES, 0, 0, tiled=True)
    owners = jnp.arange(devices, dtype=jnp.int32)[None, :]
    within = jnp.arange(nb, dtype=jnp.int32)[None, :]

    def fetch(index):
        pick = (index // nb)[:, None] == owners
        rows = jnp.dot(
            pick.astype(jnp.float32), got, precision=lax.Precision.HIGHEST
        ).reshape(index.shape[0], 6, nb)
        lanes = ((index % nb)[:, None] == within)[:, None, :]
        return jnp.sum(jnp.where(lanes, rows, 0.0), axis=2).T

    at1 = fetch(parent)
    p2 = jnp.round(at1[5]).astype(jnp.int32)
    at2 = fetch(p2)
    p3 = jnp.round(at2[5]).astype(jnp.int32)
    x0 = fetch(p3)[4]
    exit1 = at2[0] + at2[1] * bf16_round(at2[2] + at2[3] * x0)
    exit2 = at1[0] + at1[1] * bf16_round(at1[2] + at1[3] * exit1)
    r0 = bf16_round(drive0 + junction_gain * exit2)
    pressure = base + first_col * r0[:, None]
    leak = (wall_perm * (pressure - outside)).astype(jnp.bfloat16)
    destination = owner[:, 0]
    same = destination[:, None] == destination[None, :]
    earlier = jnp.arange(nb)[None, :] < jnp.arange(nb)[:, None]
    slot = jnp.sum((same & earlier).astype(jnp.int32), axis=1)
    capacity = 2
    row_of = destination * capacity + slot
    slots = devices * capacity
    onehot = row_of[None, :] == jnp.arange(slots, dtype=jnp.int32)[:, None]
    leak_sent = jnp.dot(
        onehot.astype(jnp.bfloat16), leak, preferred_element_type=jnp.float32
    ).astype(jnp.bfloat16)
    kid_sent = jnp.sum(jnp.where(onehot, kernel_id[None, :], 0), axis=1)
    tgt_sent = jnp.sum(jnp.where(onehot, target[None, :], 0), axis=1)
    cells = jnp.zeros((slots, seg), jnp.float32)
    for k in range(kernels.shape[0]):
        part = jnp.dot(leak_sent, kernels[k], preferred_element_type=jnp.float32)
        cells = jnp.where((kid_sent == k)[:, None], part, cells)
    got_rows = lax.all_to_all(
        cells.reshape(devices, capacity, seg), AXES, 0, 0, tiled=True
    ).reshape(slots, seg)
    got_index = lax.all_to_all(
        tgt_sent.astype(jnp.float32).reshape(devices, 1, capacity), AXES, 0, 0, tiled=True
    ).reshape(slots).astype(jnp.int32)
    cell_blocks = tissue_start.size // seg
    leakage = jax.ops.segment_sum(got_rows, got_index, num_segments=cell_blocks)
    leak_field = leakage.reshape(base_source.shape)
    source = base_source + leak_field
    stacked = jnp.stack([tissue_start, conduct])
    wide = padded(stacked, ((AXES, 1),), 1)
    padded_k = pad_sides(wide[1])
    partial, denominator = lax.optimization_barrier(
        relax_parts(pad_sides(wide[0]), padded_k, base_source)
    )
    first = (partial + leak_field) / denominator
    second = padded(first, ((AXES, 0),), 1)
    tissue = relax(pad_sides(second), padded_k, source)
    return (pressure, tissue)


def solution(mesh):
    in_specs = (
        P(AXES, None),
        P(AXES, None),
        P(AXES),
        P(AXES),
        P(AXES, None, None),
        P(AXES, None),
        P(AXES, None),
        P(AXES, None),
        P(AXES),
        P(AXES),
        P(),
        P(AXES, None, None),
        P(AXES, None, None),
        P(AXES, None, None),
    )
    out_specs = (P(AXES, None), P(AXES, None, None))
    return jax.shard_map(
        on_device_body, mesh=mesh, in_specs=in_specs, out_specs=out_specs, check_vma=False
    )
```

```python
import jax
import jax.numpy as jnp
from jax import lax
from jax.sharding import PartitionSpec as P

UPTAKE = 0.5
AXES = ("grp", "slab")


def padded(cells, sides, width):
    for axis, dim in sides:
        count = lax.axis_size(axis)
        ends = count - 1
        head = lax.slice_in_dim(cells, 0, width, axis=dim)
        tail = lax.slice_in_dim(cells, cells.shape[dim] - width, cells.shape[dim], axis=dim)
        cells = jnp.concatenate(
            [
                lax.ppermute(tail, axis, [(i, (i + 1) % count) for i in range(ends)]),
                cells,
                lax.ppermute(head, axis, [((i + 1) % count, i) for i in range(ends)]),
            ],
            axis=dim,
        )
    return cells


def neighbours(values):
    return [
        values[2:, 1:-1, 1:-1],
        values[:-2, 1:-1, 1:-1],
        values[1:-1, 2:, 1:-1],
        values[1:-1, :-2, 1:-1],
        values[1:-1, 1:-1, 2:],
        values[1:-1, 1:-1, :-2],
    ]


def relax(padded_p, padded_k, source):
    centre = padded_k[1:-1, 1:-1, 1:-1]
    numerator = source
    denominator = jnp.full(centre.shape, UPTAKE, jnp.float32)
    for p_side, k_side in zip(neighbours(padded_p), neighbours(padded_k)):
        facing = 0.5 * (centre + k_side)
        numerator = numerator + facing * p_side
        denominator = denominator + facing
    return numerator / denominator


def relax_parts(padded_p, padded_k, source):
    centre = padded_k[1:-1, 1:-1, 1:-1]
    numerator = source
    denominator = jnp.full(centre.shape, UPTAKE, jnp.float32)
    for p_side, k_side in zip(neighbours(padded_p), neighbours(padded_k)):
        facing = 0.5 * (centre + k_side)
        numerator = numerator + facing * p_side
        denominator = denominator + facing
    return numerator, denominator


def pad_sides(values):
    return jnp.pad(values, ((0, 0), (1, 1), (1, 1)))


def bf16_round(x):
    return x.astype(jnp.bfloat16).astype(jnp.float32)


def on_device_body(
    vessel_start,
    drive,
    junction_gain,
    parent,
    inverse_blocks,
    wall_perm,
    outside,
    owner,
    target,
    kernel_id,
    kernels,
    tissue_start,
    conduct,
    base_source,
):
    devices = lax.axis_size(AXES)
    nb = drive.shape[0]
    seg = drive.shape[1]
    lane = jnp.arange(seg, dtype=jnp.int32)[None, :]
    fixed_rhs = jnp.where(lane == 0, 0.0, drive).astype(jnp.bfloat16)
    unit = jnp.broadcast_to((lane == 0).astype(jnp.bfloat16), (nb, seg))
    both = jnp.einsum(
        "bij,cbj->cbi",
        inverse_blocks,
        jnp.stack([fixed_rhs, unit]),
        preferred_element_type=jnp.float32,
    )
    base = both[0]
    first_col = both[1]
    last_row = inverse_blocks[:, -1, :].astype(jnp.float32)
    exit_base = jnp.sum(last_row * fixed_rhs.astype(jnp.float32), axis=1)
    exit_col = last_row[:, 0]
    drive0 = drive[:, 0]
    destination = owner[:, 0]
    same = destination[:, None] == destination[None, :]
    earlier = jnp.arange(nb)[None, :] < jnp.arange(nb)[:, None]
    slot = jnp.sum((same & earlier).astype(jnp.int32), axis=1)
    capacity = 2
    row_of = destination * capacity + slot
    slots = devices * capacity
    onehot = row_of[None, :] == jnp.arange(slots, dtype=jnp.int32)[:, None]
    kid_sent = jnp.sum(jnp.where(onehot, kernel_id[None, :], 0), axis=1)
    tgt_sent = jnp.sum(jnp.where(onehot, target[None, :], 0), axis=1)
    packed = jnp.stack(
        [
            exit_base,
            exit_col,
            drive0,
            junction_gain,
            vessel_start[:, -1],
            parent.astype(jnp.float32),
        ]
    ).reshape(1, 6 * nb)
    tgt_row = jnp.pad(
        tgt_sent.astype(jnp.float32).reshape(devices, capacity),
        ((0, 0), (0, seg - capacity)),
    )
    sent = jnp.concatenate(
        [jnp.broadcast_to(packed, (devices, 6 * nb)), tgt_row], axis=1
    )
    got_all = lax.all_to_all(sent, AXES, 0, 0, tiled=True)
    got = got_all[:, : 6 * nb]
    got_index = got_all[:, 6 * nb : 6 * nb + capacity].reshape(slots).astype(jnp.int32)
    owners = jnp.arange(devices, dtype=jnp.int32)[None, :]
    within = jnp.arange(nb, dtype=jnp.int32)[None, :]

    def fetch(index):
        pick = (index // nb)[:, None] == owners
        rows = jnp.dot(
            pick.astype(jnp.float32), got, precision=lax.Precision.HIGHEST
        ).reshape(index.shape[0], 6, nb)
        lanes = ((index % nb)[:, None] == within)[:, None, :]
        return jnp.sum(jnp.where(lanes, rows, 0.0), axis=2).T

    at1 = fetch(parent)
    p2 = jnp.round(at1[5]).astype(jnp.int32)
    at2 = fetch(p2)
    p3 = jnp.round(at2[5]).astype(jnp.int32)
    x0 = fetch(p3)[4]
    exit1 = at2[0] + at2[1] * bf16_round(at2[2] + at2[3] * x0)
    exit2 = at1[0] + at1[1] * bf16_round(at1[2] + at1[3] * exit1)
    r0 = bf16_round(drive0 + junction_gain * exit2)
    pressure = base + first_col * r0[:, None]
    leak = (wall_perm * (pressure - outside)).astype(jnp.bfloat16)
    leak_sent = jnp.dot(
        onehot.astype(jnp.bfloat16), leak, preferred_element_type=jnp.float32
    ).astype(jnp.bfloat16)
    cells = jnp.zeros((slots, seg), jnp.float32)
    for k in range(kernels.shape[0]):
        part = jnp.dot(leak_sent, kernels[k], preferred_element_type=jnp.float32)
        cells = jnp.where((kid_sent == k)[:, None], part, cells)
    got_rows = lax.all_to_all(
        cells.reshape(devices, capacity, seg), AXES, 0, 0, tiled=True
    ).reshape(slots, seg)
    cell_blocks = tissue_start.size // seg
    leakage = jax.ops.segment_sum(got_rows, got_index, num_segments=cell_blocks)
    leak_field = leakage.reshape(base_source.shape)
    source = base_source + leak_field
    stacked = jnp.stack([tissue_start, conduct])
    wide = padded(stacked, ((AXES, 1),), 1)
    padded_k = pad_sides(wide[1])
    partial, denominator = lax.optimization_barrier(
        relax_parts(pad_sides(wide[0]), padded_k, base_source)
    )
    first = (partial + leak_field) / denominator
    second = padded(first, ((AXES, 0),), 1)
    tissue = relax(pad_sides(second), padded_k, source)
    return (pressure, tissue)


def solution(mesh):
    in_specs = (
        P(AXES, None),
        P(AXES, None),
        P(AXES),
        P(AXES),
        P(AXES, None, None),
        P(AXES, None),
        P(AXES, None),
        P(AXES, None),
        P(AXES),
        P(AXES),
        P(),
        P(AXES, None, None),
        P(AXES, None, None),
        P(AXES, None, None),
    )
    out_specs = (P(AXES, None), P(AXES, None, None))
    return jax.shard_map(
        on_device_body, mesh=mesh, in_specs=in_specs, out_specs=out_specs, check_vma=False
    )
```

```python
import jax
import jax.numpy as jnp
from jax import lax
from jax.sharding import PartitionSpec as P

UPTAKE = 0.5
AXES = ("grp", "slab")


def padded(cells, sides, width):
    for axis, dim in sides:
        count = lax.axis_size(axis)
        ends = count - 1
        head = lax.slice_in_dim(cells, 0, width, axis=dim)
        tail = lax.slice_in_dim(cells, cells.shape[dim] - width, cells.shape[dim], axis=dim)
        cells = jnp.concatenate(
            [
                lax.ppermute(tail, axis, [(i, (i + 1) % count) for i in range(ends)]),
                cells,
                lax.ppermute(head, axis, [((i + 1) % count, i) for i in range(ends)]),
            ],
            axis=dim,
        )
    return cells


def neighbours(values):
    return [
        values[2:, 1:-1, 1:-1],
        values[:-2, 1:-1, 1:-1],
        values[1:-1, 2:, 1:-1],
        values[1:-1, :-2, 1:-1],
        values[1:-1, 1:-1, 2:],
        values[1:-1, 1:-1, :-2],
    ]


def relax(padded_p, padded_k, source):
    centre = padded_k[1:-1, 1:-1, 1:-1]
    numerator = source
    denominator = jnp.full(centre.shape, UPTAKE, jnp.float32)
    for p_side, k_side in zip(neighbours(padded_p), neighbours(padded_k)):
        facing = 0.5 * (centre + k_side)
        numerator = numerator + facing * p_side
        denominator = denominator + facing
    return numerator / denominator


def relax_parts(padded_p, padded_k, source):
    centre = padded_k[1:-1, 1:-1, 1:-1]
    numerator = source
    denominator = jnp.full(centre.shape, UPTAKE, jnp.float32)
    for p_side, k_side in zip(neighbours(padded_p), neighbours(padded_k)):
        facing = 0.5 * (centre + k_side)
        numerator = numerator + facing * p_side
        denominator = denominator + facing
    return numerator, denominator


def pad_sides(values):
    return jnp.pad(values, ((0, 0), (1, 1), (1, 1)))


def bf16_round(x):
    return x.astype(jnp.bfloat16).astype(jnp.float32)


def on_device_body(
    vessel_start,
    drive,
    junction_gain,
    parent,
    inverse_blocks,
    wall_perm,
    outside,
    owner,
    target,
    kernel_id,
    kernels,
    tissue_start,
    conduct,
    base_source,
):
    devices = lax.axis_size(AXES)
    nb = drive.shape[0]
    seg = drive.shape[1]
    lane = jnp.arange(seg, dtype=jnp.int32)[None, :]
    fixed_rhs = jnp.where(lane == 0, 0.0, drive).astype(jnp.bfloat16)
    unit = jnp.broadcast_to((lane == 0).astype(jnp.bfloat16), (nb, seg))
    both = jnp.einsum(
        "bij,cbj->cbi",
        inverse_blocks,
        jnp.stack([fixed_rhs, unit]),
        preferred_element_type=jnp.float32,
    )
    base = both[0]
    first_col = both[1]
    last_row = inverse_blocks[:, -1, :].astype(jnp.float32)
    exit_base = jnp.sum(last_row * fixed_rhs.astype(jnp.float32), axis=1)
    exit_col = last_row[:, 0]
    drive0 = drive[:, 0]
    packed = jnp.stack(
        [
            exit_base,
            exit_col,
            drive0,
            junction_gain,
            vessel_start[:, -1],
            parent.astype(jnp.float32),
        ]
    ).reshape(1, 6 * nb)
    sent = jnp.broadcast_to(packed, (devices, 6 * nb))
    got = lax.all_to_all(sent, AXES, 0, 0, tiled=True)
    owners = jnp.arange(devices, dtype=jnp.int32)[None, :]
    within = jnp.arange(nb, dtype=jnp.int32)[None, :]

    def fetch(index):
        pick = (index // nb)[:, None] == owners
        rows = jnp.dot(
            pick.astype(jnp.float32), got, precision=lax.Precision.HIGHEST
        ).reshape(index.shape[0], 6, nb)
        lanes = ((index % nb)[:, None] == within)[:, None, :]
        return jnp.sum(jnp.where(lanes, rows, 0.0), axis=2).T

    at1 = fetch(parent)
    p2 = jnp.round(at1[5]).astype(jnp.int32)
    at2 = fetch(p2)
    p3 = jnp.round(at2[5]).astype(jnp.int32)
    x0 = fetch(p3)[4]
    exit1 = at2[0] + at2[1] * bf16_round(at2[2] + at2[3] * x0)
    exit2 = at1[0] + at1[1] * bf16_round(at1[2] + at1[3] * exit1)
    r0 = bf16_round(drive0 + junction_gain * exit2)
    pressure = base + first_col * r0[:, None]
    leak = (wall_perm * (pressure - outside)).astype(jnp.bfloat16)
    destination = owner[:, 0]
    same = destination[:, None] == destination[None, :]
    earlier = jnp.arange(nb)[None, :] < jnp.arange(nb)[:, None]
    slot = jnp.sum((same & earlier).astype(jnp.int32), axis=1)
    capacity = 2
    row_of = destination * capacity + slot
    slots = devices * capacity
    onehot = row_of[None, :] == jnp.arange(slots, dtype=jnp.int32)[:, None]
    leak_sent = jnp.dot(
        onehot.astype(jnp.bfloat16), leak, preferred_element_type=jnp.float32
    ).astype(jnp.bfloat16)
    kid_sent = jnp.sum(jnp.where(onehot, kernel_id[None, :], 0), axis=1)
    tgt_sent = jnp.sum(jnp.where(onehot, target[None, :], 0), axis=1)
    cells = jnp.zeros((slots, seg), jnp.float32)
    for k in range(kernels.shape[0]):
        part = jnp.dot(leak_sent, kernels[k], preferred_element_type=jnp.float32)
        cells = jnp.where((kid_sent == k)[:, None], part, cells)
    tgt_row = jnp.pad(
        tgt_sent.astype(jnp.float32).reshape(devices, 1, capacity),
        ((0, 0), (0, capacity - 1), (0, seg - capacity)),
    )
    send = jnp.concatenate([cells.reshape(devices, capacity, seg), tgt_row], axis=1)
    recv = lax.all_to_all(send, AXES, 0, 0, tiled=True)
    got_rows = recv[:, :capacity, :].reshape(slots, seg)
    got_index = recv[:, capacity, :capacity].reshape(slots).astype(jnp.int32)
    cell_blocks = tissue_start.size // seg
    leakage = jax.ops.segment_sum(got_rows, got_index, num_segments=cell_blocks)
    leak_field = leakage.reshape(base_source.shape)
    source = base_source + leak_field
    stacked = jnp.stack([tissue_start, conduct])
    wide = padded(stacked, ((AXES, 1),), 1)
    padded_k = pad_sides(wide[1])
    partial, denominator = lax.optimization_barrier(
        relax_parts(pad_sides(wide[0]), padded_k, base_source)
    )
    first = (partial + leak_field) / denominator
    second = padded(first, ((AXES, 0),), 1)
    tissue = relax(pad_sides(second), padded_k, source)
    return (pressure, tissue)


def solution(mesh):
    in_specs = (
        P(AXES, None),
        P(AXES, None),
        P(AXES),
        P(AXES),
        P(AXES, None, None),
        P(AXES, None),
        P(AXES, None),
        P(AXES, None),
        P(AXES),
        P(AXES),
        P(),
        P(AXES, None, None),
        P(AXES, None, None),
        P(AXES, None, None),
    )
    out_specs = (P(AXES, None), P(AXES, None, None))
    return jax.shard_map(
        on_device_body, mesh=mesh, in_specs=in_specs, out_specs=out_specs, check_vma=False
    )
```

```python
import jax
import jax.numpy as jnp
from jax import lax
from jax.sharding import PartitionSpec as P

UPTAKE = 0.5
AXES = ("grp", "slab")


def padded(cells, sides, width):
    for axis, dim in sides:
        count = lax.axis_size(axis)
        ends = count - 1
        head = lax.slice_in_dim(cells, 0, width, axis=dim)
        tail = lax.slice_in_dim(cells, cells.shape[dim] - width, cells.shape[dim], axis=dim)
        cells = jnp.concatenate(
            [
                lax.ppermute(tail, axis, [(i, (i + 1) % count) for i in range(ends)]),
                cells,
                lax.ppermute(head, axis, [((i + 1) % count, i) for i in range(ends)]),
            ],
            axis=dim,
        )
    return cells


def neighbours(values):
    return [
        values[2:, 1:-1, 1:-1],
        values[:-2, 1:-1, 1:-1],
        values[1:-1, 2:, 1:-1],
        values[1:-1, :-2, 1:-1],
        values[1:-1, 1:-1, 2:],
        values[1:-1, 1:-1, :-2],
    ]


def relax(padded_p, padded_k, source):
    centre = padded_k[1:-1, 1:-1, 1:-1]
    numerator = source
    denominator = jnp.full(centre.shape, UPTAKE, jnp.float32)
    for p_side, k_side in zip(neighbours(padded_p), neighbours(padded_k)):
        facing = 0.5 * (centre + k_side)
        numerator = numerator + facing * p_side
        denominator = denominator + facing
    return numerator / denominator


def relax_parts(padded_p, padded_k, source):
    centre = padded_k[1:-1, 1:-1, 1:-1]
    numerator = source
    denominator = jnp.full(centre.shape, UPTAKE, jnp.float32)
    for p_side, k_side in zip(neighbours(padded_p), neighbours(padded_k)):
        facing = 0.5 * (centre + k_side)
        numerator = numerator + facing * p_side
        denominator = denominator + facing
    return numerator, denominator


def pad_sides(values):
    return jnp.pad(values, ((0, 0), (1, 1), (1, 1)))


def bf16_round(x):
    return x.astype(jnp.bfloat16).astype(jnp.float32)


def on_device(
    vessel_start,
    drive,
    junction_gain,
    parent,
    inverse_blocks,
    wall_perm,
    outside,
    owner,
    target,
    kernel_id,
    kernels,
    tissue_start,
    conduct,
    base_source,
):
    devices = lax.axis_size(AXES)
    nb = drive.shape[0]
    seg = drive.shape[1]
    lane = jnp.arange(seg, dtype=jnp.int32)[None, :]
    fixed_rhs = jnp.where(lane == 0, 0.0, drive).astype(jnp.bfloat16)
    unit = jnp.broadcast_to((lane == 0).astype(jnp.bfloat16), (nb, seg))
    both = jnp.einsum(
        "bij,cbj->cbi",
        inverse_blocks,
        jnp.stack([fixed_rhs, unit]),
        preferred_element_type=jnp.float32,
    )
    base = both[0]
    first_col = both[1]
    last_row = inverse_blocks[:, -1, :].astype(jnp.float32)
    exit_base = jnp.sum(last_row * fixed_rhs.astype(jnp.float32), axis=1)
    exit_col = last_row[:, 0]
    drive0 = drive[:, 0]
    packed = jnp.stack(
        [
            exit_base,
            exit_col,
            drive0,
            junction_gain,
            vessel_start[:, -1],
            parent.astype(jnp.float32),
        ]
    ).reshape(1, 6 * nb)
    sent = jnp.broadcast_to(packed, (devices, 6 * nb))
    got = lax.all_to_all(sent, AXES, 0, 0, tiled=True)
    owners = jnp.arange(devices, dtype=jnp.int32)[None, :]
    within = jnp.arange(nb, dtype=jnp.int32)[None, :]

    def fetch(index):
        pick = (index // nb)[:, None] == owners
        rows = jnp.dot(
            pick.astype(jnp.float32), got, precision=lax.Precision.HIGHEST
        ).reshape(index.shape[0], 6, nb)
        lanes = ((index % nb)[:, None] == within)[:, None, :]
        return jnp.sum(jnp.where(lanes, rows, 0.0), axis=2).T

    at1 = fetch(parent)
    p2 = jnp.round(at1[5]).astype(jnp.int32)
    at2 = fetch(p2)
    p3 = jnp.round(at2[5]).astype(jnp.int32)
    x0 = fetch(p3)[4]
    exit1 = at2[0] + at2[1] * bf16_round(at2[2] + at2[3] * x0)
    exit2 = at1[0] + at1[1] * bf16_round(at1[2] + at1[3] * exit1)
    r0 = bf16_round(drive0 + junction_gain * exit2)
    pressure = base + first_col * r0[:, None]
    leak = (wall_perm * (pressure - outside)).astype(jnp.bfloat16)
    destination = owner[:, 0]
    same = destination[:, None] == destination[None, :]
    earlier = jnp.arange(nb)[None, :] < jnp.arange(nb)[:, None]
    slot = jnp.sum((same & earlier).astype(jnp.int32), axis=1)
    capacity = 2
    row_of = destination * capacity + slot
    slots = devices * capacity
    onehot = row_of[None, :] == jnp.arange(slots, dtype=jnp.int32)[:, None]
    leak_sent = jnp.dot(
        onehot.astype(jnp.bfloat16), leak, preferred_element_type=jnp.float32
    ).astype(jnp.bfloat16)
    kid_sent = jnp.sum(jnp.where(onehot, kernel_id[None, :], 0), axis=1)
    tgt_sent = jnp.sum(jnp.where(onehot, target[None, :], 0), axis=1)
    cells = jnp.zeros((slots, seg), jnp.float32)
    for k in range(kernels.shape[0]):
        part = jnp.dot(leak_sent, kernels[k], preferred_element_type=jnp.float32)
        cells = jnp.where((kid_sent == k)[:, None], part, cells)
    tgt_row = jnp.pad(
        tgt_sent.astype(jnp.float32).reshape(devices, capacity), ((0, 0), (0, seg - capacity))
    )
    send = jnp.concatenate(
        [cells.reshape(devices, capacity, seg), tgt_row[:, None, :]], axis=1
    )
    recv = lax.all_to_all(
        send.reshape(devices, (capacity + 1) * seg), AXES, 0, 0, tiled=True
    ).reshape(devices, capacity + 1, seg)
    got_rows = recv[:, :capacity, :].reshape(slots, seg)
    got_index = recv[:, capacity, :capacity].reshape(slots).astype(jnp.int32)
    per_row = base_source.shape[2] // seg
    plane_rows = base_source.shape[0] * base_source.shape[1]
    spots = (got_index % per_row)[:, None] == jnp.arange(per_row, dtype=jnp.int32)[None, :]
    placed = jnp.where(spots[:, :, None], got_rows[:, None, :], 0.0).reshape(
        slots, per_row * seg
    )
    rows_hit = (got_index // per_row)[None, :] == jnp.arange(plane_rows, dtype=jnp.int32)[:, None]
    leak_field = jnp.dot(
        rows_hit.astype(jnp.float32), placed, precision=lax.Precision.HIGHEST
    ).reshape(base_source.shape)
    source = base_source + leak_field
    stacked = jnp.stack([tissue_start, conduct])
    wide = padded(stacked, ((AXES, 1),), 1)
    padded_k = pad_sides(wide[1])
    partial, denominator = relax_parts(pad_sides(wide[0]), padded_k, base_source)
    first = (partial + leak_field) / denominator
    second = padded(first, ((AXES, 0),), 1)
    tissue = relax(pad_sides(second), padded_k, source)
    return (pressure, tissue)


def solution(mesh):
    in_specs = (
        P(AXES, None),
        P(AXES, None),
        P(AXES),
        P(AXES),
        P(AXES, None, None),
        P(AXES, None),
        P(AXES, None),
        P(AXES, None),
        P(AXES),
        P(AXES),
        P(),
        P(AXES, None, None),
        P(AXES, None, None),
        P(AXES, None, None),
    )
    out_specs = (P(AXES, None), P(AXES, None, None))
    return jax.shard_map(
        on_device, mesh=mesh, in_specs=in_specs, out_specs=out_specs, check_vma=False
    )
```

```python
import jax
import jax.numpy as jnp
from jax import lax
from jax.sharding import PartitionSpec as P

UPTAKE = 0.5
AXES = ("grp", "slab")


def padded(cells, sides, width):
    for axis, dim in sides:
        count = lax.axis_size(axis)
        ends = count - 1
        head = lax.slice_in_dim(cells, 0, width, axis=dim)
        tail = lax.slice_in_dim(cells, cells.shape[dim] - width, cells.shape[dim], axis=dim)
        cells = jnp.concatenate(
            [
                lax.ppermute(tail, axis, [(i, (i + 1) % count) for i in range(ends)]),
                cells,
                lax.ppermute(head, axis, [((i + 1) % count, i) for i in range(ends)]),
            ],
            axis=dim,
        )
    return cells


def shifted(values, axis, step):
    size = values.shape[axis]
    widths = [(0, 0)] * values.ndim
    if step > 0:
        body = lax.slice_in_dim(values, 1, size, axis=axis)
        widths[axis] = (0, 1)
    else:
        body = lax.slice_in_dim(values, 0, size - 1, axis=axis)
        widths[axis] = (1, 0)
    return jnp.pad(body, widths)


def neighbours(values):
    inner = values[1:-1]
    return [
        values[2:],
        values[:-2],
        shifted(inner, 1, 1),
        shifted(inner, 1, -1),
        shifted(inner, 2, 1),
        shifted(inner, 2, -1),
    ]


def relax(padded_p, padded_k, source):
    centre = padded_k[1:-1]
    numerator = source
    denominator = jnp.full(centre.shape, UPTAKE, jnp.float32)
    for p_side, k_side in zip(neighbours(padded_p), neighbours(padded_k)):
        facing = 0.5 * (centre + k_side)
        numerator = numerator + facing * p_side
        denominator = denominator + facing
    return numerator / denominator


def relax_parts(padded_p, padded_k, source):
    centre = padded_k[1:-1]
    numerator = source
    denominator = jnp.full(centre.shape, UPTAKE, jnp.float32)
    for p_side, k_side in zip(neighbours(padded_p), neighbours(padded_k)):
        facing = 0.5 * (centre + k_side)
        numerator = numerator + facing * p_side
        denominator = denominator + facing
    return numerator, denominator


def pad_sides(values):
    return jnp.pad(values, ((0, 0), (1, 1), (1, 1)))


def bf16_round(x):
    return x.astype(jnp.bfloat16).astype(jnp.float32)


def on_device(
    vessel_start,
    drive,
    junction_gain,
    parent,
    inverse_blocks,
    wall_perm,
    outside,
    owner,
    target,
    kernel_id,
    kernels,
    tissue_start,
    conduct,
    base_source,
):
    devices = lax.axis_size(AXES)
    nb = drive.shape[0]
    seg = drive.shape[1]
    lane = jnp.arange(seg, dtype=jnp.int32)[None, :]
    fixed_rhs = jnp.where(lane == 0, 0.0, drive).astype(jnp.bfloat16)
    unit = jnp.broadcast_to((lane == 0).astype(jnp.bfloat16), (nb, seg))
    both = jnp.einsum(
        "bij,cbj->cbi",
        inverse_blocks,
        jnp.stack([fixed_rhs, unit]),
        preferred_element_type=jnp.float32,
    )
    base = both[0]
    first_col = both[1]
    last_row = inverse_blocks[:, -1, :].astype(jnp.float32)
    exit_base = jnp.sum(last_row * fixed_rhs.astype(jnp.float32), axis=1)
    exit_col = last_row[:, 0]
    drive0 = drive[:, 0]
    packed = jnp.stack(
        [
            exit_base,
            exit_col,
            drive0,
            junction_gain,
            vessel_start[:, -1],
            parent.astype(jnp.float32),
        ]
    ).reshape(1, 6 * nb)
    sent = jnp.broadcast_to(packed, (devices, 6 * nb))
    got = lax.all_to_all(sent, AXES, 0, 0, tiled=True)
    owners = jnp.arange(devices, dtype=jnp.int32)[None, :]
    within = jnp.arange(nb, dtype=jnp.int32)[None, :]

    def fetch(index):
        pick = (index // nb)[:, None] == owners
        rows = jnp.dot(
            pick.astype(jnp.float32), got, precision=lax.Precision.HIGHEST
        ).reshape(index.shape[0], 6, nb)
        lanes = ((index % nb)[:, None] == within)[:, None, :]
        return jnp.sum(jnp.where(lanes, rows, 0.0), axis=2).T

    at1 = fetch(parent)
    p2 = jnp.round(at1[5]).astype(jnp.int32)
    at2 = fetch(p2)
    p3 = jnp.round(at2[5]).astype(jnp.int32)
    x0 = fetch(p3)[4]
    exit1 = at2[0] + at2[1] * bf16_round(at2[2] + at2[3] * x0)
    exit2 = at1[0] + at1[1] * bf16_round(at1[2] + at1[3] * exit1)
    r0 = bf16_round(drive0 + junction_gain * exit2)
    pressure = base + first_col * r0[:, None]
    leak = (wall_perm * (pressure - outside)).astype(jnp.bfloat16)
    destination = owner[:, 0]
    same = destination[:, None] == destination[None, :]
    earlier = jnp.arange(nb)[None, :] < jnp.arange(nb)[:, None]
    slot = jnp.sum((same & earlier).astype(jnp.int32), axis=1)
    capacity = 2
    row_of = destination * capacity + slot
    slots = devices * capacity
    onehot = row_of[None, :] == jnp.arange(slots, dtype=jnp.int32)[:, None]
    leak_sent = jnp.dot(
        onehot.astype(jnp.bfloat16), leak, preferred_element_type=jnp.float32
    ).astype(jnp.bfloat16)
    kid_sent = jnp.sum(jnp.where(onehot, kernel_id[None, :], 0), axis=1)
    tgt_sent = jnp.sum(jnp.where(onehot, target[None, :], 0), axis=1)
    cells = jnp.zeros((slots, seg), jnp.float32)
    for k in range(kernels.shape[0]):
        part = jnp.dot(leak_sent, kernels[k], preferred_element_type=jnp.float32)
        cells = jnp.where((kid_sent == k)[:, None], part, cells)
    tgt_row = jnp.pad(
        tgt_sent.astype(jnp.float32).reshape(devices, capacity), ((0, 0), (0, seg - capacity))
    )
    send = jnp.concatenate(
        [cells.reshape(devices, capacity, seg), tgt_row[:, None, :]], axis=1
    )
    recv = lax.all_to_all(
        send.reshape(devices, (capacity + 1) * seg), AXES, 0, 0, tiled=True
    ).reshape(devices, capacity + 1, seg)
    got_rows = recv[:, :capacity, :].reshape(slots, seg)
    got_index = recv[:, capacity, :capacity].reshape(slots).astype(jnp.int32)
    cell_blocks = tissue_start.size // seg
    leakage = jax.ops.segment_sum(got_rows, got_index, num_segments=cell_blocks)
    leak_field = leakage.reshape(base_source.shape)
    source = base_source + leak_field
    stacked = jnp.stack([tissue_start, conduct])
    wide = padded(stacked, ((AXES, 1),), 1)
    padded_k = wide[1]
    partial, denominator = relax_parts(wide[0], padded_k, base_source)
    first = (partial + leak_field) / denominator
    second = padded(first, ((AXES, 0),), 1)
    tissue = relax(second, padded_k, source)
    return (pressure, tissue)


def solution(mesh):
    in_specs = (
        P(AXES, None),
        P(AXES, None),
        P(AXES),
        P(AXES),
        P(AXES, None, None),
        P(AXES, None),
        P(AXES, None),
        P(AXES, None),
        P(AXES),
        P(AXES),
        P(),
        P(AXES, None, None),
        P(AXES, None, None),
        P(AXES, None, None),
    )
    out_specs = (P(AXES, None), P(AXES, None, None))
    return jax.shard_map(
        on_device, mesh=mesh, in_specs=in_specs, out_specs=out_specs, check_vma=False
    )
```

```python
import jax
import jax.numpy as jnp
from jax import lax
from jax.sharding import PartitionSpec as P
from jax.experimental import pallas as pl
from jax.experimental.pallas import tpu as pltpu

UPTAKE = 0.5
AXES = ("grp", "slab")


def padded(cells, sides, width):
    for axis, dim in sides:
        count = lax.axis_size(axis)
        ends = count - 1
        head = lax.slice_in_dim(cells, 0, width, axis=dim)
        tail = lax.slice_in_dim(cells, cells.shape[dim] - width, cells.shape[dim], axis=dim)
        cells = jnp.concatenate(
            [
                lax.ppermute(tail, axis, [(i, (i + 1) % count) for i in range(ends)]),
                cells,
                lax.ppermute(head, axis, [((i + 1) % count, i) for i in range(ends)]),
            ],
            axis=dim,
        )
    return cells


def neighbours(values):
    return [
        values[2:, 1:-1, 1:-1],
        values[:-2, 1:-1, 1:-1],
        values[1:-1, 2:, 1:-1],
        values[1:-1, :-2, 1:-1],
        values[1:-1, 1:-1, 2:],
        values[1:-1, 1:-1, :-2],
    ]


def relax(padded_p, padded_k, source):
    centre = padded_k[1:-1, 1:-1, 1:-1]
    numerator = source
    denominator = jnp.full(centre.shape, UPTAKE, jnp.float32)
    for p_side, k_side in zip(neighbours(padded_p), neighbours(padded_k)):
        facing = 0.5 * (centre + k_side)
        numerator = numerator + facing * p_side
        denominator = denominator + facing
    return numerator / denominator


def relax_parts(padded_p, padded_k, source):
    centre = padded_k[1:-1, 1:-1, 1:-1]
    numerator = source
    denominator = jnp.full(centre.shape, UPTAKE, jnp.float32)
    for p_side, k_side in zip(neighbours(padded_p), neighbours(padded_k)):
        facing = 0.5 * (centre + k_side)
        numerator = numerator + facing * p_side
        denominator = denominator + facing
    return numerator, denominator


def _relax_kernel(pm, pc, pp, km, kc, kp, src, out):
    p = pc[0]
    k = kc[0]
    rows, cols = p.shape
    row = jax.lax.broadcasted_iota(jnp.int32, (rows, cols), 0)
    col = jax.lax.broadcasted_iota(jnp.int32, (rows, cols), 1)

    def side(v, axis, step, edge):
        size = v.shape[axis]
        moved = pltpu.roll(v, (size - step) % size, axis)
        return jnp.where(edge, 0.0, moved)

    x_hi = row == rows - 1
    x_lo = row == 0
    y_hi = col == cols - 1
    y_lo = col == 0
    sides = [
        (pp[0], kp[0]),
        (pm[0], km[0]),
        (side(p, 0, 1, x_hi), side(k, 0, 1, x_hi)),
        (side(p, 0, -1, x_lo), side(k, 0, -1, x_lo)),
        (side(p, 1, 1, y_hi), side(k, 1, 1, y_hi)),
        (side(p, 1, -1, y_lo), side(k, 1, -1, y_lo)),
    ]
    numerator = src[0]
    denominator = jnp.full(p.shape, UPTAKE, jnp.float32)
    for p_side, k_side in sides:
        facing = 0.5 * (k + k_side)
        numerator = numerator + facing * p_side
        denominator = denominator + facing
    out[0] = numerator / denominator


def relax_sweep(p_halo, k_halo, source):
    planes, rows, cols = source.shape
    block = (1, rows, cols)
    at = lambda shift: pl.BlockSpec(block, lambda z: (z + shift, 0, 0))
    return pl.pallas_call(
        _relax_kernel,
        grid=(planes,),
        in_specs=[at(0), at(1), at(2), at(0), at(1), at(2), at(0)],
        out_specs=at(0),
        out_shape=jax.ShapeDtypeStruct(source.shape, jnp.float32),
    )(p_halo, p_halo, p_halo, k_halo, k_halo, k_halo, source)


def pad_sides(values):
    return jnp.pad(values, ((0, 0), (1, 1), (1, 1)))


def bf16_round(x):
    return x.astype(jnp.bfloat16).astype(jnp.float32)


def on_device(
    vessel_start,
    drive,
    junction_gain,
    parent,
    inverse_blocks,
    wall_perm,
    outside,
    owner,
    target,
    kernel_id,
    kernels,
    tissue_start,
    conduct,
    base_source,
):
    devices = lax.axis_size(AXES)
    nb = drive.shape[0]
    seg = drive.shape[1]
    lane = jnp.arange(seg, dtype=jnp.int32)[None, :]
    fixed_rhs = jnp.where(lane == 0, 0.0, drive).astype(jnp.bfloat16)
    unit = jnp.broadcast_to((lane == 0).astype(jnp.bfloat16), (nb, seg))
    both = jnp.einsum(
        "bij,cbj->cbi",
        inverse_blocks,
        jnp.stack([fixed_rhs, unit]),
        preferred_element_type=jnp.float32,
    )
    base = both[0]
    first_col = both[1]
    last_row = inverse_blocks[:, -1, :].astype(jnp.float32)
    exit_base = jnp.sum(last_row * fixed_rhs.astype(jnp.float32), axis=1)
    exit_col = last_row[:, 0]
    drive0 = drive[:, 0]
    packed = jnp.stack(
        [
            exit_base,
            exit_col,
            drive0,
            junction_gain,
            vessel_start[:, -1],
            parent.astype(jnp.float32),
        ]
    ).reshape(1, 6 * nb)
    sent = jnp.broadcast_to(packed, (devices, 6 * nb))
    got = lax.all_to_all(sent, AXES, 0, 0, tiled=True)
    owners = jnp.arange(devices, dtype=jnp.int32)[None, :]
    within = jnp.arange(nb, dtype=jnp.int32)[None, :]

    def fetch(index):
        pick = (index // nb)[:, None] == owners
        rows = jnp.dot(
            pick.astype(jnp.float32), got, precision=lax.Precision.HIGHEST
        ).reshape(index.shape[0], 6, nb)
        lanes = ((index % nb)[:, None] == within)[:, None, :]
        return jnp.sum(jnp.where(lanes, rows, 0.0), axis=2).T

    at1 = fetch(parent)
    p2 = jnp.round(at1[5]).astype(jnp.int32)
    at2 = fetch(p2)
    p3 = jnp.round(at2[5]).astype(jnp.int32)
    x0 = fetch(p3)[4]
    exit1 = at2[0] + at2[1] * bf16_round(at2[2] + at2[3] * x0)
    exit2 = at1[0] + at1[1] * bf16_round(at1[2] + at1[3] * exit1)
    r0 = bf16_round(drive0 + junction_gain * exit2)
    pressure = base + first_col * r0[:, None]
    leak = (wall_perm * (pressure - outside)).astype(jnp.bfloat16)
    destination = owner[:, 0]
    same = destination[:, None] == destination[None, :]
    earlier = jnp.arange(nb)[None, :] < jnp.arange(nb)[:, None]
    slot = jnp.sum((same & earlier).astype(jnp.int32), axis=1)
    capacity = 2
    row_of = destination * capacity + slot
    slots = devices * capacity
    onehot = row_of[None, :] == jnp.arange(slots, dtype=jnp.int32)[:, None]
    leak_sent = jnp.dot(
        onehot.astype(jnp.bfloat16), leak, preferred_element_type=jnp.float32
    ).astype(jnp.bfloat16)
    kid_sent = jnp.sum(jnp.where(onehot, kernel_id[None, :], 0), axis=1)
    tgt_sent = jnp.sum(jnp.where(onehot, target[None, :], 0), axis=1)
    cells = jnp.zeros((slots, seg), jnp.float32)
    for k in range(kernels.shape[0]):
        part = jnp.dot(leak_sent, kernels[k], preferred_element_type=jnp.float32)
        cells = jnp.where((kid_sent == k)[:, None], part, cells)
    tgt_row = jnp.pad(
        tgt_sent.astype(jnp.float32).reshape(devices, capacity), ((0, 0), (0, seg - capacity))
    )
    send = jnp.concatenate(
        [cells.reshape(devices, capacity, seg), tgt_row[:, None, :]], axis=1
    )
    recv = lax.all_to_all(
        send.reshape(devices, (capacity + 1) * seg), AXES, 0, 0, tiled=True
    ).reshape(devices, capacity + 1, seg)
    got_rows = recv[:, :capacity, :].reshape(slots, seg)
    got_index = recv[:, capacity, :capacity].reshape(slots).astype(jnp.int32)
    cell_blocks = tissue_start.size // seg
    leakage = jax.ops.segment_sum(got_rows, got_index, num_segments=cell_blocks)
    source = base_source + leakage.reshape(base_source.shape)
    stacked = jnp.stack([tissue_start, conduct])
    wide = padded(stacked, ((AXES, 1),), 1)
    first = relax_sweep(wide[0], wide[1], source)
    second = padded(first, ((AXES, 0),), 1)
    tissue = relax_sweep(second, wide[1], source)
    return (pressure, tissue)


def solution(mesh):
    in_specs = (
        P(AXES, None),
        P(AXES, None),
        P(AXES),
        P(AXES),
        P(AXES, None, None),
        P(AXES, None),
        P(AXES, None),
        P(AXES, None),
        P(AXES),
        P(AXES),
        P(),
        P(AXES, None, None),
        P(AXES, None, None),
        P(AXES, None, None),
    )
    out_specs = (P(AXES, None), P(AXES, None, None))
    return jax.shard_map(
        on_device, mesh=mesh, in_specs=in_specs, out_specs=out_specs, check_vma=False
    )
```

```python
import jax
import jax.numpy as jnp
from jax import lax
from jax.sharding import PartitionSpec as P
from jax.experimental import pallas as pl
from jax.experimental.pallas import tpu as pltpu

UPTAKE = 0.5
AXES = ("grp", "slab")


def padded(cells, sides, width):
    for axis, dim in sides:
        count = lax.axis_size(axis)
        ends = count - 1
        head = lax.slice_in_dim(cells, 0, width, axis=dim)
        tail = lax.slice_in_dim(cells, cells.shape[dim] - width, cells.shape[dim], axis=dim)
        cells = jnp.concatenate(
            [
                lax.ppermute(tail, axis, [(i, (i + 1) % count) for i in range(ends)]),
                cells,
                lax.ppermute(head, axis, [((i + 1) % count, i) for i in range(ends)]),
            ],
            axis=dim,
        )
    return cells


def neighbours(values):
    return [
        values[2:, 1:-1, 1:-1],
        values[:-2, 1:-1, 1:-1],
        values[1:-1, 2:, 1:-1],
        values[1:-1, :-2, 1:-1],
        values[1:-1, 1:-1, 2:],
        values[1:-1, 1:-1, :-2],
    ]


def relax(padded_p, padded_k, source):
    centre = padded_k[1:-1, 1:-1, 1:-1]
    numerator = source
    denominator = jnp.full(centre.shape, UPTAKE, jnp.float32)
    for p_side, k_side in zip(neighbours(padded_p), neighbours(padded_k)):
        facing = 0.5 * (centre + k_side)
        numerator = numerator + facing * p_side
        denominator = denominator + facing
    return numerator / denominator


def relax_parts(padded_p, padded_k, source):
    centre = padded_k[1:-1, 1:-1, 1:-1]
    numerator = source
    denominator = jnp.full(centre.shape, UPTAKE, jnp.float32)
    for p_side, k_side in zip(neighbours(padded_p), neighbours(padded_k)):
        facing = 0.5 * (centre + k_side)
        numerator = numerator + facing * p_side
        denominator = denominator + facing
    return numerator, denominator


def _relax_kernel(p_ref, p_lo, p_hi, k_ref, k_lo, k_hi, base, leak, out):
    z = pl.program_id(0)
    top = p_ref.shape[0] - 1
    p = p_ref[z]
    k = k_ref[z]
    up = jnp.minimum(z + 1, top)
    down = jnp.maximum(z - 1, 0)
    p_up = jnp.where(z == top, p_hi[0], p_ref[up])
    k_up = jnp.where(z == top, k_hi[0], k_ref[up])
    p_down = jnp.where(z == 0, p_lo[0], p_ref[down])
    k_down = jnp.where(z == 0, k_lo[0], k_ref[down])
    rows, cols = p.shape
    row = jax.lax.broadcasted_iota(jnp.int32, (rows, cols), 0)
    col = jax.lax.broadcasted_iota(jnp.int32, (rows, cols), 1)

    def side(v, axis, step, edge):
        size = v.shape[axis]
        moved = pltpu.roll(v, (size - step) % size, axis)
        return jnp.where(edge, 0.0, moved)

    x_hi = row == rows - 1
    x_lo = row == 0
    y_hi = col == cols - 1
    y_lo = col == 0
    sides = [
        (p_up, k_up),
        (p_down, k_down),
        (side(p, 0, 1, x_hi), side(k, 0, 1, x_hi)),
        (side(p, 0, -1, x_lo), side(k, 0, -1, x_lo)),
        (side(p, 1, 1, y_hi), side(k, 1, 1, y_hi)),
        (side(p, 1, -1, y_lo), side(k, 1, -1, y_lo)),
    ]
    numerator = base[0] + leak[0]
    denominator = jnp.full(p.shape, UPTAKE, jnp.float32)
    for p_side, k_side in sides:
        facing = 0.5 * (k + k_side)
        numerator = numerator + facing * p_side
        denominator = denominator + facing
    out[0] = numerator / denominator


def relax_sweep(p, p_lo, p_hi, k, k_lo, k_hi, base, leak):
    planes, rows, cols = base.shape
    whole = pl.BlockSpec((planes, rows, cols), lambda z: (0, 0, 0))
    one = pl.BlockSpec((1, rows, cols), lambda z: (0, 0, 0))
    plane = pl.BlockSpec((1, rows, cols), lambda z: (z, 0, 0))
    return pl.pallas_call(
        _relax_kernel,
        grid=(planes,),
        in_specs=[whole, one, one, whole, one, one, plane, plane],
        out_specs=plane,
        out_shape=jax.ShapeDtypeStruct(base.shape, jnp.float32),
    )(p, p_lo, p_hi, k, k_lo, k_hi, base, leak)


def halos(cells):
    count = lax.axis_size(AXES)
    ends = count - 1
    last = cells.shape[1] - 1
    lo = lax.ppermute(cells[:, last:], AXES, [(i, i + 1) for i in range(ends)])
    hi = lax.ppermute(cells[:, :1], AXES, [(i + 1, i) for i in range(ends)])
    return lo, hi


def pad_sides(values):
    return jnp.pad(values, ((0, 0), (1, 1), (1, 1)))


def bf16_round(x):
    return x.astype(jnp.bfloat16).astype(jnp.float32)


def on_device(
    vessel_start,
    drive,
    junction_gain,
    parent,
    inverse_blocks,
    wall_perm,
    outside,
    owner,
    target,
    kernel_id,
    kernels,
    tissue_start,
    conduct,
    base_source,
):
    devices = lax.axis_size(AXES)
    nb = drive.shape[0]
    seg = drive.shape[1]
    lane = jnp.arange(seg, dtype=jnp.int32)[None, :]
    fixed_rhs = jnp.where(lane == 0, 0.0, drive).astype(jnp.bfloat16)
    unit = jnp.broadcast_to((lane == 0).astype(jnp.bfloat16), (nb, seg))
    both = jnp.einsum(
        "bij,cbj->cbi",
        inverse_blocks,
        jnp.stack([fixed_rhs, unit]),
        preferred_element_type=jnp.float32,
    )
    base = both[0]
    first_col = both[1]
    last_row = inverse_blocks[:, -1, :].astype(jnp.float32)
    exit_base = jnp.sum(last_row * fixed_rhs.astype(jnp.float32), axis=1)
    exit_col = last_row[:, 0]
    drive0 = drive[:, 0]
    packed = jnp.stack(
        [
            exit_base,
            exit_col,
            drive0,
            junction_gain,
            vessel_start[:, -1],
            parent.astype(jnp.float32),
        ]
    ).reshape(1, 6 * nb)
    sent = jnp.broadcast_to(packed, (devices, 6 * nb))
    got = lax.all_to_all(sent, AXES, 0, 0, tiled=True)
    owners = jnp.arange(devices, dtype=jnp.int32)[None, :]
    within = jnp.arange(nb, dtype=jnp.int32)[None, :]

    def fetch(index):
        pick = (index // nb)[:, None] == owners
        rows = jnp.dot(
            pick.astype(jnp.float32), got, precision=lax.Precision.HIGHEST
        ).reshape(index.shape[0], 6, nb)
        lanes = ((index % nb)[:, None] == within)[:, None, :]
        return jnp.sum(jnp.where(lanes, rows, 0.0), axis=2).T

    at1 = fetch(parent)
    p2 = jnp.round(at1[5]).astype(jnp.int32)
    at2 = fetch(p2)
    p3 = jnp.round(at2[5]).astype(jnp.int32)
    x0 = fetch(p3)[4]
    exit1 = at2[0] + at2[1] * bf16_round(at2[2] + at2[3] * x0)
    exit2 = at1[0] + at1[1] * bf16_round(at1[2] + at1[3] * exit1)
    r0 = bf16_round(drive0 + junction_gain * exit2)
    pressure = base + first_col * r0[:, None]
    leak = (wall_perm * (pressure - outside)).astype(jnp.bfloat16)
    destination = owner[:, 0]
    same = destination[:, None] == destination[None, :]
    earlier = jnp.arange(nb)[None, :] < jnp.arange(nb)[:, None]
    slot = jnp.sum((same & earlier).astype(jnp.int32), axis=1)
    capacity = 2
    row_of = destination * capacity + slot
    slots = devices * capacity
    onehot = row_of[None, :] == jnp.arange(slots, dtype=jnp.int32)[:, None]
    leak_sent = jnp.dot(
        onehot.astype(jnp.bfloat16), leak, preferred_element_type=jnp.float32
    ).astype(jnp.bfloat16)
    kid_sent = jnp.sum(jnp.where(onehot, kernel_id[None, :], 0), axis=1)
    tgt_sent = jnp.sum(jnp.where(onehot, target[None, :], 0), axis=1)
    cells = jnp.zeros((slots, seg), jnp.float32)
    for k in range(kernels.shape[0]):
        part = jnp.dot(leak_sent, kernels[k], preferred_element_type=jnp.float32)
        cells = jnp.where((kid_sent == k)[:, None], part, cells)
    tgt_row = jnp.pad(
        tgt_sent.astype(jnp.float32).reshape(devices, capacity), ((0, 0), (0, seg - capacity))
    )
    send = jnp.concatenate(
        [cells.reshape(devices, capacity, seg), tgt_row[:, None, :]], axis=1
    )
    recv = lax.all_to_all(
        send.reshape(devices, (capacity + 1) * seg), AXES, 0, 0, tiled=True
    ).reshape(devices, capacity + 1, seg)
    got_rows = recv[:, :capacity, :].reshape(slots, seg)
    got_index = recv[:, capacity, :capacity].reshape(slots).astype(jnp.int32)
    cell_blocks = tissue_start.size // seg
    leakage = jax.ops.segment_sum(got_rows, got_index, num_segments=cell_blocks)
    leak_field = leakage.reshape(base_source.shape)
    lo, hi = halos(jnp.stack([tissue_start, conduct]))
    first = relax_sweep(
        tissue_start, lo[0], hi[0], conduct, lo[1], hi[1], base_source, leak_field
    )
    first_lo, first_hi = halos(first[None])
    tissue = relax_sweep(
        first, first_lo[0], first_hi[0], conduct, lo[1], hi[1], base_source, leak_field
    )
    return (pressure, tissue)


def solution(mesh):
    in_specs = (
        P(AXES, None),
        P(AXES, None),
        P(AXES),
        P(AXES),
        P(AXES, None, None),
        P(AXES, None),
        P(AXES, None),
        P(AXES, None),
        P(AXES),
        P(AXES),
        P(),
        P(AXES, None, None),
        P(AXES, None, None),
        P(AXES, None, None),
    )
    out_specs = (P(AXES, None), P(AXES, None, None))
    return jax.shard_map(
        on_device, mesh=mesh, in_specs=in_specs, out_specs=out_specs, check_vma=False
    )
```

```python
import jax
import jax.numpy as jnp
from jax import lax
from jax.sharding import PartitionSpec as P
from jax.experimental import pallas as pl
from jax.experimental.pallas import tpu as pltpu

UPTAKE = 0.5
AXES = ("grp", "slab")


def padded(cells, sides, width):
    for axis, dim in sides:
        count = lax.axis_size(axis)
        ends = count - 1
        head = lax.slice_in_dim(cells, 0, width, axis=dim)
        tail = lax.slice_in_dim(cells, cells.shape[dim] - width, cells.shape[dim], axis=dim)
        cells = jnp.concatenate(
            [
                lax.ppermute(tail, axis, [(i, (i + 1) % count) for i in range(ends)]),
                cells,
                lax.ppermute(head, axis, [((i + 1) % count, i) for i in range(ends)]),
            ],
            axis=dim,
        )
    return cells


def neighbours(values):
    return [
        values[2:, 1:-1, 1:-1],
        values[:-2, 1:-1, 1:-1],
        values[1:-1, 2:, 1:-1],
        values[1:-1, :-2, 1:-1],
        values[1:-1, 1:-1, 2:],
        values[1:-1, 1:-1, :-2],
    ]


def relax(padded_p, padded_k, source):
    centre = padded_k[1:-1, 1:-1, 1:-1]
    numerator = source
    denominator = jnp.full(centre.shape, UPTAKE, jnp.float32)
    for p_side, k_side in zip(neighbours(padded_p), neighbours(padded_k)):
        facing = 0.5 * (centre + k_side)
        numerator = numerator + facing * p_side
        denominator = denominator + facing
    return numerator / denominator


def relax_parts(padded_p, padded_k, source):
    centre = padded_k[1:-1, 1:-1, 1:-1]
    numerator = source
    denominator = jnp.full(centre.shape, UPTAKE, jnp.float32)
    for p_side, k_side in zip(neighbours(padded_p), neighbours(padded_k)):
        facing = 0.5 * (centre + k_side)
        numerator = numerator + facing * p_side
        denominator = denominator + facing
    return numerator, denominator


def _relax_kernel(p_ref, p_lo, p_hi, k_ref, k_lo, k_hi, base, leak, out):
    z = pl.program_id(0)
    top = p_ref.shape[0] - 1
    p = p_ref[z]
    k = k_ref[z]
    up = jnp.minimum(z + 1, top)
    down = jnp.maximum(z - 1, 0)
    p_up = jnp.where(z == top, p_hi[0], p_ref[up])
    k_up = jnp.where(z == top, k_hi[0], k_ref[up])
    p_down = jnp.where(z == 0, p_lo[0], p_ref[down])
    k_down = jnp.where(z == 0, k_lo[0], k_ref[down])
    rows, cols = p.shape
    row = jax.lax.broadcasted_iota(jnp.int32, (rows, cols), 0)
    col = jax.lax.broadcasted_iota(jnp.int32, (rows, cols), 1)

    def side(v, axis, step, edge):
        size = v.shape[axis]
        moved = pltpu.roll(v, (size - step) % size, axis)
        return jnp.where(edge, 0.0, moved)

    x_hi = row == rows - 1
    x_lo = row == 0
    y_hi = col == cols - 1
    y_lo = col == 0
    sides = [
        (p_up, k_up),
        (p_down, k_down),
        (side(p, 0, 1, x_hi), side(k, 0, 1, x_hi)),
        (side(p, 0, -1, x_lo), side(k, 0, -1, x_lo)),
        (side(p, 1, 1, y_hi), side(k, 1, 1, y_hi)),
        (side(p, 1, -1, y_lo), side(k, 1, -1, y_lo)),
    ]
    numerator = base[0] + leak[0]
    denominator = jnp.full(p.shape, UPTAKE, jnp.float32)
    for p_side, k_side in sides:
        facing = 0.5 * (k + k_side)
        numerator = numerator + facing * p_side
        denominator = denominator + facing
    out[0] = numerator / denominator


def relax_sweep(p, p_lo, p_hi, p_at, k, k_lo, k_hi, k_at, base, leak):
    planes, rows, cols = base.shape
    whole = pl.BlockSpec((planes, rows, cols), lambda z: (0, 0, 0))
    plane = pl.BlockSpec((1, rows, cols), lambda z: (z, 0, 0))

    def edge(at):
        return pl.BlockSpec((None, 1, rows, cols), lambda z: (at, 0, 0, 0))

    return pl.pallas_call(
        _relax_kernel,
        grid=(planes,),
        in_specs=[whole, edge(p_at), edge(p_at), whole, edge(k_at), edge(k_at), plane, plane],
        out_specs=plane,
        out_shape=jax.ShapeDtypeStruct(base.shape, jnp.float32),
    )(p, p_lo, p_hi, k, k_lo, k_hi, base, leak)


def halos(cells):
    count = lax.axis_size(AXES)
    ends = count - 1
    last = cells.shape[1] - 1
    lo = lax.ppermute(cells[:, last:], AXES, [(i, i + 1) for i in range(ends)])
    hi = lax.ppermute(cells[:, :1], AXES, [(i + 1, i) for i in range(ends)])
    return lo, hi


def pad_sides(values):
    return jnp.pad(values, ((0, 0), (1, 1), (1, 1)))


def bf16_round(x):
    return x.astype(jnp.bfloat16).astype(jnp.float32)


def on_device(
    vessel_start,
    drive,
    junction_gain,
    parent,
    inverse_blocks,
    wall_perm,
    outside,
    owner,
    target,
    kernel_id,
    kernels,
    tissue_start,
    conduct,
    base_source,
):
    devices = lax.axis_size(AXES)
    nb = drive.shape[0]
    seg = drive.shape[1]
    lane = jnp.arange(seg, dtype=jnp.int32)[None, :]
    fixed_rhs = jnp.where(lane == 0, 0.0, drive).astype(jnp.bfloat16)
    unit = jnp.broadcast_to((lane == 0).astype(jnp.bfloat16), (nb, seg))
    both = jnp.einsum(
        "bij,cbj->cbi",
        inverse_blocks,
        jnp.stack([fixed_rhs, unit]),
        preferred_element_type=jnp.float32,
    )
    base = both[0]
    first_col = both[1]
    last_row = inverse_blocks[:, -1, :].astype(jnp.float32)
    exit_base = jnp.sum(last_row * fixed_rhs.astype(jnp.float32), axis=1)
    exit_col = last_row[:, 0]
    drive0 = drive[:, 0]
    packed = jnp.stack(
        [
            exit_base,
            exit_col,
            drive0,
            junction_gain,
            vessel_start[:, -1],
            parent.astype(jnp.float32),
        ]
    ).reshape(1, 6 * nb)
    sent = jnp.broadcast_to(packed, (devices, 6 * nb))
    got = lax.all_to_all(sent, AXES, 0, 0, tiled=True)
    owners = jnp.arange(devices, dtype=jnp.int32)[None, :]
    within = jnp.arange(nb, dtype=jnp.int32)[None, :]

    def fetch(index):
        pick = (index // nb)[:, None] == owners
        rows = jnp.dot(
            pick.astype(jnp.float32), got, precision=lax.Precision.HIGHEST
        ).reshape(index.shape[0], 6, nb)
        lanes = ((index % nb)[:, None] == within)[:, None, :]
        return jnp.sum(jnp.where(lanes, rows, 0.0), axis=2).T

    at1 = fetch(parent)
    p2 = jnp.round(at1[5]).astype(jnp.int32)
    at2 = fetch(p2)
    p3 = jnp.round(at2[5]).astype(jnp.int32)
    x0 = fetch(p3)[4]
    exit1 = at2[0] + at2[1] * bf16_round(at2[2] + at2[3] * x0)
    exit2 = at1[0] + at1[1] * bf16_round(at1[2] + at1[3] * exit1)
    r0 = bf16_round(drive0 + junction_gain * exit2)
    pressure = base + first_col * r0[:, None]
    leak = (wall_perm * (pressure - outside)).astype(jnp.bfloat16)
    destination = owner[:, 0]
    same = destination[:, None] == destination[None, :]
    earlier = jnp.arange(nb)[None, :] < jnp.arange(nb)[:, None]
    slot = jnp.sum((same & earlier).astype(jnp.int32), axis=1)
    capacity = 2
    row_of = destination * capacity + slot
    slots = devices * capacity
    onehot = row_of[None, :] == jnp.arange(slots, dtype=jnp.int32)[:, None]
    leak_sent = jnp.dot(
        onehot.astype(jnp.bfloat16), leak, preferred_element_type=jnp.float32
    ).astype(jnp.bfloat16)
    kid_sent = jnp.sum(jnp.where(onehot, kernel_id[None, :], 0), axis=1)
    tgt_sent = jnp.sum(jnp.where(onehot, target[None, :], 0), axis=1)
    cells = jnp.zeros((slots, seg), jnp.float32)
    for k in range(kernels.shape[0]):
        part = jnp.dot(leak_sent, kernels[k], preferred_element_type=jnp.float32)
        cells = jnp.where((kid_sent == k)[:, None], part, cells)
    tgt_row = jnp.pad(
        tgt_sent.astype(jnp.float32).reshape(devices, capacity), ((0, 0), (0, seg - capacity))
    )
    send = jnp.concatenate(
        [cells.reshape(devices, capacity, seg), tgt_row[:, None, :]], axis=1
    )
    recv = lax.all_to_all(
        send.reshape(devices, (capacity + 1) * seg), AXES, 0, 0, tiled=True
    ).reshape(devices, capacity + 1, seg)
    got_rows = recv[:, :capacity, :].reshape(slots, seg)
    got_index = recv[:, capacity, :capacity].reshape(slots).astype(jnp.int32)
    cell_blocks = tissue_start.size // seg
    leakage = jax.ops.segment_sum(got_rows, got_index, num_segments=cell_blocks)
    leak_field = leakage.reshape(base_source.shape)
    lo, hi = halos(jnp.stack([tissue_start, conduct]))
    first = relax_sweep(
        tissue_start, lo, hi, 0, conduct, lo, hi, 1, base_source, leak_field
    )
    first_lo, first_hi = halos(first[None])
    tissue = relax_sweep(
        first, first_lo, first_hi, 0, conduct, lo, hi, 1, base_source, leak_field
    )
    return (pressure, tissue)


def solution(mesh):
    in_specs = (
        P(AXES, None),
        P(AXES, None),
        P(AXES),
        P(AXES),
        P(AXES, None, None),
        P(AXES, None),
        P(AXES, None),
        P(AXES, None),
        P(AXES),
        P(AXES),
        P(),
        P(AXES, None, None),
        P(AXES, None, None),
        P(AXES, None, None),
    )
    out_specs = (P(AXES, None), P(AXES, None, None))
    return jax.shard_map(
        on_device, mesh=mesh, in_specs=in_specs, out_specs=out_specs, check_vma=False
    )
```

```python
import functools

import jax
import jax.numpy as jnp
from jax import lax
from jax.sharding import PartitionSpec as P
from jax.experimental import pallas as pl
from jax.experimental.pallas import tpu as pltpu

UPTAKE = 0.5
AXES = ("grp", "slab")


def padded(cells, sides, width):
    for axis, dim in sides:
        count = lax.axis_size(axis)
        ends = count - 1
        head = lax.slice_in_dim(cells, 0, width, axis=dim)
        tail = lax.slice_in_dim(cells, cells.shape[dim] - width, cells.shape[dim], axis=dim)
        cells = jnp.concatenate(
            [
                lax.ppermute(tail, axis, [(i, (i + 1) % count) for i in range(ends)]),
                cells,
                lax.ppermute(head, axis, [((i + 1) % count, i) for i in range(ends)]),
            ],
            axis=dim,
        )
    return cells


def neighbours(values):
    return [
        values[2:, 1:-1, 1:-1],
        values[:-2, 1:-1, 1:-1],
        values[1:-1, 2:, 1:-1],
        values[1:-1, :-2, 1:-1],
        values[1:-1, 1:-1, 2:],
        values[1:-1, 1:-1, :-2],
    ]


def relax(padded_p, padded_k, source):
    centre = padded_k[1:-1, 1:-1, 1:-1]
    numerator = source
    denominator = jnp.full(centre.shape, UPTAKE, jnp.float32)
    for p_side, k_side in zip(neighbours(padded_p), neighbours(padded_k)):
        facing = 0.5 * (centre + k_side)
        numerator = numerator + facing * p_side
        denominator = denominator + facing
    return numerator / denominator


def relax_parts(padded_p, padded_k, source):
    centre = padded_k[1:-1, 1:-1, 1:-1]
    numerator = source
    denominator = jnp.full(centre.shape, UPTAKE, jnp.float32)
    for p_side, k_side in zip(neighbours(padded_p), neighbours(padded_k)):
        facing = 0.5 * (centre + k_side)
        numerator = numerator + facing * p_side
        denominator = denominator + facing
    return numerator, denominator


def _relax_kernel(plane_of, p_ref, p_lo, p_hi, k_ref, k_lo, k_hi, base, leak, out):
    z = plane_of(pl.program_id(0))
    top = p_ref.shape[0] - 1
    p = p_ref[z]
    k = k_ref[z]
    up = jnp.minimum(z + 1, top)
    down = jnp.maximum(z - 1, 0)
    p_up = jnp.where(z == top, p_hi[0], p_ref[up])
    k_up = jnp.where(z == top, k_hi[0], k_ref[up])
    p_down = jnp.where(z == 0, p_lo[0], p_ref[down])
    k_down = jnp.where(z == 0, k_lo[0], k_ref[down])
    rows, cols = p.shape
    row = jax.lax.broadcasted_iota(jnp.int32, (rows, cols), 0)
    col = jax.lax.broadcasted_iota(jnp.int32, (rows, cols), 1)

    def side(v, axis, step, edge):
        size = v.shape[axis]
        moved = pltpu.roll(v, (size - step) % size, axis)
        return jnp.where(edge, 0.0, moved)

    x_hi = row == rows - 1
    x_lo = row == 0
    y_hi = col == cols - 1
    y_lo = col == 0
    sides = [
        (p_up, k_up),
        (p_down, k_down),
        (side(p, 0, 1, x_hi), side(k, 0, 1, x_hi)),
        (side(p, 0, -1, x_lo), side(k, 0, -1, x_lo)),
        (side(p, 1, 1, y_hi), side(k, 1, 1, y_hi)),
        (side(p, 1, -1, y_lo), side(k, 1, -1, y_lo)),
    ]
    numerator = base[0] + leak[0]
    denominator = jnp.full(p.shape, UPTAKE, jnp.float32)
    for p_side, k_side in sides:
        facing = 0.5 * (k + k_side)
        numerator = numerator + facing * p_side
        denominator = denominator + facing
    out[0] = numerator / denominator


def relax_sweep(p, p_lo, p_hi, p_at, k, k_lo, k_hi, k_at, base, leak, plane_of, count):
    planes, rows, cols = base.shape
    whole = pl.BlockSpec((planes, rows, cols), lambda z: (0, 0, 0))
    plane = pl.BlockSpec((1, rows, cols), lambda z: (plane_of(z), 0, 0))
    step = pl.BlockSpec((1, rows, cols), lambda z: (z, 0, 0))

    def edge(at):
        return pl.BlockSpec((None, 1, rows, cols), lambda z: (at, 0, 0, 0))

    return pl.pallas_call(
        functools.partial(_relax_kernel, plane_of),
        grid=(count,),
        in_specs=[whole, edge(p_at), edge(p_at), whole, edge(k_at), edge(k_at), plane, plane],
        out_specs=step,
        out_shape=jax.ShapeDtypeStruct((count, rows, cols), jnp.float32),
    )(p, p_lo, p_hi, k, k_lo, k_hi, base, leak)


def halos(cells):
    count = lax.axis_size(AXES)
    ends = count - 1
    last = cells.shape[1] - 1
    lo = lax.ppermute(cells[:, last:], AXES, [(i, i + 1) for i in range(ends)])
    hi = lax.ppermute(cells[:, :1], AXES, [(i + 1, i) for i in range(ends)])
    return lo, hi


def pad_sides(values):
    return jnp.pad(values, ((0, 0), (1, 1), (1, 1)))


def bf16_round(x):
    return x.astype(jnp.bfloat16).astype(jnp.float32)


def on_device(
    vessel_start,
    drive,
    junction_gain,
    parent,
    inverse_blocks,
    wall_perm,
    outside,
    owner,
    target,
    kernel_id,
    kernels,
    tissue_start,
    conduct,
    base_source,
):
    devices = lax.axis_size(AXES)
    nb = drive.shape[0]
    seg = drive.shape[1]
    lane = jnp.arange(seg, dtype=jnp.int32)[None, :]
    fixed_rhs = jnp.where(lane == 0, 0.0, drive).astype(jnp.bfloat16)
    unit = jnp.broadcast_to((lane == 0).astype(jnp.bfloat16), (nb, seg))
    both = jnp.einsum(
        "bij,cbj->cbi",
        inverse_blocks,
        jnp.stack([fixed_rhs, unit]),
        preferred_element_type=jnp.float32,
    )
    base = both[0]
    first_col = both[1]
    last_row = inverse_blocks[:, -1, :].astype(jnp.float32)
    exit_base = jnp.sum(last_row * fixed_rhs.astype(jnp.float32), axis=1)
    exit_col = last_row[:, 0]
    drive0 = drive[:, 0]
    packed = jnp.stack(
        [
            exit_base,
            exit_col,
            drive0,
            junction_gain,
            vessel_start[:, -1],
            parent.astype(jnp.float32),
        ]
    ).reshape(1, 6 * nb)
    sent = jnp.broadcast_to(packed, (devices, 6 * nb))
    got = lax.all_to_all(sent, AXES, 0, 0, tiled=True)
    owners = jnp.arange(devices, dtype=jnp.int32)[None, :]
    within = jnp.arange(nb, dtype=jnp.int32)[None, :]

    def fetch(index):
        pick = (index // nb)[:, None] == owners
        rows = jnp.dot(
            pick.astype(jnp.float32), got, precision=lax.Precision.HIGHEST
        ).reshape(index.shape[0], 6, nb)
        lanes = ((index % nb)[:, None] == within)[:, None, :]
        return jnp.sum(jnp.where(lanes, rows, 0.0), axis=2).T

    at1 = fetch(parent)
    p2 = jnp.round(at1[5]).astype(jnp.int32)
    at2 = fetch(p2)
    p3 = jnp.round(at2[5]).astype(jnp.int32)
    x0 = fetch(p3)[4]
    exit1 = at2[0] + at2[1] * bf16_round(at2[2] + at2[3] * x0)
    exit2 = at1[0] + at1[1] * bf16_round(at1[2] + at1[3] * exit1)
    r0 = bf16_round(drive0 + junction_gain * exit2)
    pressure = base + first_col * r0[:, None]
    leak = (wall_perm * (pressure - outside)).astype(jnp.bfloat16)
    destination = owner[:, 0]
    same = destination[:, None] == destination[None, :]
    earlier = jnp.arange(nb)[None, :] < jnp.arange(nb)[:, None]
    slot = jnp.sum((same & earlier).astype(jnp.int32), axis=1)
    capacity = 2
    row_of = destination * capacity + slot
    slots = devices * capacity
    onehot = row_of[None, :] == jnp.arange(slots, dtype=jnp.int32)[:, None]
    leak_sent = jnp.dot(
        onehot.astype(jnp.bfloat16), leak, preferred_element_type=jnp.float32
    ).astype(jnp.bfloat16)
    kid_sent = jnp.sum(jnp.where(onehot, kernel_id[None, :], 0), axis=1)
    tgt_sent = jnp.sum(jnp.where(onehot, target[None, :], 0), axis=1)
    cells = jnp.zeros((slots, seg), jnp.float32)
    for k in range(kernels.shape[0]):
        part = jnp.dot(leak_sent, kernels[k], preferred_element_type=jnp.float32)
        cells = jnp.where((kid_sent == k)[:, None], part, cells)
    tgt_row = jnp.pad(
        tgt_sent.astype(jnp.float32).reshape(devices, capacity), ((0, 0), (0, seg - capacity))
    )
    send = jnp.concatenate(
        [cells.reshape(devices, capacity, seg), tgt_row[:, None, :]], axis=1
    )
    recv = lax.all_to_all(
        send.reshape(devices, (capacity + 1) * seg), AXES, 0, 0, tiled=True
    ).reshape(devices, capacity + 1, seg)
    got_rows = recv[:, :capacity, :].reshape(slots, seg)
    got_index = recv[:, capacity, :capacity].reshape(slots).astype(jnp.int32)
    cell_blocks = tissue_start.size // seg
    leakage = jax.ops.segment_sum(got_rows, got_index, num_segments=cell_blocks)
    leak_field = leakage.reshape(base_source.shape)
    lo, hi = halos(jnp.stack([tissue_start, conduct]))
    planes = base_source.shape[0]
    args = (tissue_start, lo, hi, 0, conduct, lo, hi, 1, base_source, leak_field)
    ends = relax_sweep(*args, lambda z: z * (planes - 1), 2)
    first_lo, first_hi = halos(ends[None])
    inner = relax_sweep(*args, lambda z: z + 1, planes - 2)
    first = jnp.concatenate([ends[0:1], inner, ends[1:2]], axis=0)
    tissue = relax_sweep(
        first, first_lo, first_hi, 0, conduct, lo, hi, 1, base_source, leak_field,
        lambda z: z, planes,
    )
    return (pressure, tissue)


def solution(mesh):
    in_specs = (
        P(AXES, None),
        P(AXES, None),
        P(AXES),
        P(AXES),
        P(AXES, None, None),
        P(AXES, None),
        P(AXES, None),
        P(AXES, None),
        P(AXES),
        P(AXES),
        P(),
        P(AXES, None, None),
        P(AXES, None, None),
        P(AXES, None, None),
    )
    out_specs = (P(AXES, None), P(AXES, None, None))
    return jax.shard_map(
        on_device, mesh=mesh, in_specs=in_specs, out_specs=out_specs, check_vma=False
    )
```

```python
import functools

import jax
import jax.numpy as jnp
from jax import lax
from jax.sharding import PartitionSpec as P
from jax.experimental import pallas as pl
from jax.experimental.pallas import tpu as pltpu

UPTAKE = 0.5
AXES = ("grp", "slab")


def padded(cells, sides, width):
    for axis, dim in sides:
        count = lax.axis_size(axis)
        ends = count - 1
        head = lax.slice_in_dim(cells, 0, width, axis=dim)
        tail = lax.slice_in_dim(cells, cells.shape[dim] - width, cells.shape[dim], axis=dim)
        cells = jnp.concatenate(
            [
                lax.ppermute(tail, axis, [(i, (i + 1) % count) for i in range(ends)]),
                cells,
                lax.ppermute(head, axis, [((i + 1) % count, i) for i in range(ends)]),
            ],
            axis=dim,
        )
    return cells


def neighbours(values):
    return [
        values[2:, 1:-1, 1:-1],
        values[:-2, 1:-1, 1:-1],
        values[1:-1, 2:, 1:-1],
        values[1:-1, :-2, 1:-1],
        values[1:-1, 1:-1, 2:],
        values[1:-1, 1:-1, :-2],
    ]


def relax(padded_p, padded_k, source):
    centre = padded_k[1:-1, 1:-1, 1:-1]
    numerator = source
    denominator = jnp.full(centre.shape, UPTAKE, jnp.float32)
    for p_side, k_side in zip(neighbours(padded_p), neighbours(padded_k)):
        facing = 0.5 * (centre + k_side)
        numerator = numerator + facing * p_side
        denominator = denominator + facing
    return numerator / denominator


def relax_parts(padded_p, padded_k, source):
    centre = padded_k[1:-1, 1:-1, 1:-1]
    numerator = source
    denominator = jnp.full(centre.shape, UPTAKE, jnp.float32)
    for p_side, k_side in zip(neighbours(padded_p), neighbours(padded_k)):
        facing = 0.5 * (centre + k_side)
        numerator = numerator + facing * p_side
        denominator = denominator + facing
    return numerator, denominator


def _relax_kernel(plane_of, mode, p_ref, p_lo, p_hi, k_ref, k_lo, k_hi, base, leak, *rest):
    z = plane_of(pl.program_id(0))
    top = p_ref.shape[0] - 1
    p = p_ref[z]
    k = k_ref[z]
    up = jnp.minimum(z + 1, top)
    down = jnp.maximum(z - 1, 0)
    p_up = jnp.where(z == top, p_hi[0], p_ref[up])
    k_up = jnp.where(z == top, k_hi[0], k_ref[up])
    p_down = jnp.where(z == 0, p_lo[0], p_ref[down])
    k_down = jnp.where(z == 0, k_lo[0], k_ref[down])
    rows, cols = p.shape
    row = jax.lax.broadcasted_iota(jnp.int32, (rows, cols), 0)
    col = jax.lax.broadcasted_iota(jnp.int32, (rows, cols), 1)

    def side(v, axis, step, edge):
        size = v.shape[axis]
        moved = pltpu.roll(v, (size - step) % size, axis)
        return jnp.where(edge, 0.0, moved)

    x_hi = row == rows - 1
    x_lo = row == 0
    y_hi = col == cols - 1
    y_lo = col == 0
    sides = [
        (p_up, k_up),
        (p_down, k_down),
        (side(p, 0, 1, x_hi), side(k, 0, 1, x_hi)),
        (side(p, 0, -1, x_lo), side(k, 0, -1, x_lo)),
        (side(p, 1, 1, y_hi), side(k, 1, 1, y_hi)),
        (side(p, 1, -1, y_lo), side(k, 1, -1, y_lo)),
    ]
    numerator = base[0] + leak[0]
    denominator = jnp.full(p.shape, UPTAKE, jnp.float32)
    for p_side, k_side in sides:
        facing = 0.5 * (k + k_side)
        numerator = numerator + facing * p_side
        if mode == 0:
            denominator = denominator + facing
    if mode == 0:
        out, den = rest
        den[0] = denominator
    else:
        den_ends, den_inner, out = rest
        on_edge = (z == 0) | (z == top)
        denominator = jnp.where(on_edge, den_ends[0], den_inner[0])
    out[0] = numerator / denominator


def relax_sweep(p, p_lo, p_hi, p_at, k, k_lo, k_hi, k_at, base, leak, plane_of, count, dens=None):
    planes, rows, cols = base.shape
    whole = pl.BlockSpec((planes, rows, cols), lambda z: (0, 0, 0))
    plane = pl.BlockSpec((1, rows, cols), lambda z: (plane_of(z), 0, 0))
    step = pl.BlockSpec((1, rows, cols), lambda z: (z, 0, 0))

    def edge(at):
        return pl.BlockSpec((None, 1, rows, cols), lambda z: (at, 0, 0, 0))

    specs = [whole, edge(p_at), edge(p_at), whole, edge(k_at), edge(k_at), plane, plane]
    shape = jax.ShapeDtypeStruct((count, rows, cols), jnp.float32)
    operands = (p, p_lo, p_hi, k, k_lo, k_hi, base, leak)
    if dens is None:
        return pl.pallas_call(
            functools.partial(_relax_kernel, plane_of, 0),
            grid=(count,),
            in_specs=specs,
            out_specs=(step, step),
            out_shape=(shape, shape),
        )(*operands)
    top = planes - 1
    end_at = pl.BlockSpec((1, rows, cols), lambda z: (jnp.minimum(plane_of(z), 1), 0, 0))
    inner_at = pl.BlockSpec(
        (1, rows, cols), lambda z: (jnp.clip(plane_of(z) - 1, 0, top - 2), 0, 0)
    )
    return pl.pallas_call(
        functools.partial(_relax_kernel, plane_of, 1),
        grid=(count,),
        in_specs=specs + [end_at, inner_at],
        out_specs=step,
        out_shape=shape,
    )(*operands, *dens)


def halos(cells):
    count = lax.axis_size(AXES)
    ends = count - 1
    last = cells.shape[1] - 1
    lo = lax.ppermute(cells[:, last:], AXES, [(i, i + 1) for i in range(ends)])
    hi = lax.ppermute(cells[:, :1], AXES, [(i + 1, i) for i in range(ends)])
    return lo, hi


def pad_sides(values):
    return jnp.pad(values, ((0, 0), (1, 1), (1, 1)))


def bf16_round(x):
    return x.astype(jnp.bfloat16).astype(jnp.float32)


def on_device(
    vessel_start,
    drive,
    junction_gain,
    parent,
    inverse_blocks,
    wall_perm,
    outside,
    owner,
    target,
    kernel_id,
    kernels,
    tissue_start,
    conduct,
    base_source,
):
    devices = lax.axis_size(AXES)
    nb = drive.shape[0]
    seg = drive.shape[1]
    lane = jnp.arange(seg, dtype=jnp.int32)[None, :]
    fixed_rhs = jnp.where(lane == 0, 0.0, drive).astype(jnp.bfloat16)
    unit = jnp.broadcast_to((lane == 0).astype(jnp.bfloat16), (nb, seg))
    both = jnp.einsum(
        "bij,cbj->cbi",
        inverse_blocks,
        jnp.stack([fixed_rhs, unit]),
        preferred_element_type=jnp.float32,
    )
    base = both[0]
    first_col = both[1]
    last_row = inverse_blocks[:, -1, :].astype(jnp.float32)
    exit_base = jnp.sum(last_row * fixed_rhs.astype(jnp.float32), axis=1)
    exit_col = last_row[:, 0]
    drive0 = drive[:, 0]
    packed = jnp.stack(
        [
            exit_base,
            exit_col,
            drive0,
            junction_gain,
            vessel_start[:, -1],
            parent.astype(jnp.float32),
        ]
    ).reshape(1, 6 * nb)
    sent = jnp.broadcast_to(packed, (devices, 6 * nb))
    got = lax.all_to_all(sent, AXES, 0, 0, tiled=True)
    owners = jnp.arange(devices, dtype=jnp.int32)[None, :]
    within = jnp.arange(nb, dtype=jnp.int32)[None, :]

    def fetch(index):
        pick = (index // nb)[:, None] == owners
        rows = jnp.dot(
            pick.astype(jnp.float32), got, precision=lax.Precision.HIGHEST
        ).reshape(index.shape[0], 6, nb)
        lanes = ((index % nb)[:, None] == within)[:, None, :]
        return jnp.sum(jnp.where(lanes, rows, 0.0), axis=2).T

    at1 = fetch(parent)
    p2 = jnp.round(at1[5]).astype(jnp.int32)
    at2 = fetch(p2)
    p3 = jnp.round(at2[5]).astype(jnp.int32)
    x0 = fetch(p3)[4]
    exit1 = at2[0] + at2[1] * bf16_round(at2[2] + at2[3] * x0)
    exit2 = at1[0] + at1[1] * bf16_round(at1[2] + at1[3] * exit1)
    r0 = bf16_round(drive0 + junction_gain * exit2)
    pressure = base + first_col * r0[:, None]
    leak = (wall_perm * (pressure - outside)).astype(jnp.bfloat16)
    destination = owner[:, 0]
    same = destination[:, None] == destination[None, :]
    earlier = jnp.arange(nb)[None, :] < jnp.arange(nb)[:, None]
    slot = jnp.sum((same & earlier).astype(jnp.int32), axis=1)
    capacity = 2
    row_of = destination * capacity + slot
    slots = devices * capacity
    onehot = row_of[None, :] == jnp.arange(slots, dtype=jnp.int32)[:, None]
    leak_sent = jnp.dot(
        onehot.astype(jnp.bfloat16), leak, preferred_element_type=jnp.float32
    ).astype(jnp.bfloat16)
    kid_sent = jnp.sum(jnp.where(onehot, kernel_id[None, :], 0), axis=1)
    tgt_sent = jnp.sum(jnp.where(onehot, target[None, :], 0), axis=1)
    cells = jnp.zeros((slots, seg), jnp.float32)
    for k in range(kernels.shape[0]):
        part = jnp.dot(leak_sent, kernels[k], preferred_element_type=jnp.float32)
        cells = jnp.where((kid_sent == k)[:, None], part, cells)
    tgt_row = jnp.pad(
        tgt_sent.astype(jnp.float32).reshape(devices, capacity), ((0, 0), (0, seg - capacity))
    )
    send = jnp.concatenate(
        [cells.reshape(devices, capacity, seg), tgt_row[:, None, :]], axis=1
    )
    recv = lax.all_to_all(
        send.reshape(devices, (capacity + 1) * seg), AXES, 0, 0, tiled=True
    ).reshape(devices, capacity + 1, seg)
    got_rows = recv[:, :capacity, :].reshape(slots, seg)
    got_index = recv[:, capacity, :capacity].reshape(slots).astype(jnp.int32)
    cell_blocks = tissue_start.size // seg
    leakage = jax.ops.segment_sum(got_rows, got_index, num_segments=cell_blocks)
    leak_field = leakage.reshape(base_source.shape)
    lo, hi = halos(jnp.stack([tissue_start, conduct]))
    planes = base_source.shape[0]
    args = (tissue_start, lo, hi, 0, conduct, lo, hi, 1, base_source, leak_field)
    ends, den_ends = relax_sweep(*args, lambda z: z * (planes - 1), 2)
    first_lo, first_hi = halos(ends[None])
    inner, den_inner = relax_sweep(*args, lambda z: z + 1, planes - 2)
    first = jnp.concatenate([ends[0:1], inner, ends[1:2]], axis=0)
    tissue = relax_sweep(
        first, first_lo, first_hi, 0, conduct, lo, hi, 1, base_source, leak_field,
        lambda z: z, planes, (den_ends, den_inner),
    )
    return (pressure, tissue)


def solution(mesh):
    in_specs = (
        P(AXES, None),
        P(AXES, None),
        P(AXES),
        P(AXES),
        P(AXES, None, None),
        P(AXES, None),
        P(AXES, None),
        P(AXES, None),
        P(AXES),
        P(AXES),
        P(),
        P(AXES, None, None),
        P(AXES, None, None),
        P(AXES, None, None),
    )
    out_specs = (P(AXES, None), P(AXES, None, None))
    return jax.shard_map(
        on_device, mesh=mesh, in_specs=in_specs, out_specs=out_specs, check_vma=False
    )
```

```python
import functools

import jax
import jax.numpy as jnp
from jax import lax
from jax.sharding import PartitionSpec as P
from jax.experimental import pallas as pl
from jax.experimental.pallas import tpu as pltpu

UPTAKE = 0.5
AXES = ("grp", "slab")


def padded(cells, sides, width):
    for axis, dim in sides:
        count = lax.axis_size(axis)
        ends = count - 1
        head = lax.slice_in_dim(cells, 0, width, axis=dim)
        tail = lax.slice_in_dim(cells, cells.shape[dim] - width, cells.shape[dim], axis=dim)
        cells = jnp.concatenate(
            [
                lax.ppermute(tail, axis, [(i, (i + 1) % count) for i in range(ends)]),
                cells,
                lax.ppermute(head, axis, [((i + 1) % count, i) for i in range(ends)]),
            ],
            axis=dim,
        )
    return cells


def neighbours(values):
    return [
        values[2:, 1:-1, 1:-1],
        values[:-2, 1:-1, 1:-1],
        values[1:-1, 2:, 1:-1],
        values[1:-1, :-2, 1:-1],
        values[1:-1, 1:-1, 2:],
        values[1:-1, 1:-1, :-2],
    ]


def relax(padded_p, padded_k, source):
    centre = padded_k[1:-1, 1:-1, 1:-1]
    numerator = source
    denominator = jnp.full(centre.shape, UPTAKE, jnp.float32)
    for p_side, k_side in zip(neighbours(padded_p), neighbours(padded_k)):
        facing = 0.5 * (centre + k_side)
        numerator = numerator + facing * p_side
        denominator = denominator + facing
    return numerator / denominator


def relax_parts(padded_p, padded_k, source):
    centre = padded_k[1:-1, 1:-1, 1:-1]
    numerator = source
    denominator = jnp.full(centre.shape, UPTAKE, jnp.float32)
    for p_side, k_side in zip(neighbours(padded_p), neighbours(padded_k)):
        facing = 0.5 * (centre + k_side)
        numerator = numerator + facing * p_side
        denominator = denominator + facing
    return numerator, denominator


def _relax_kernel(plane_of, p_ref, p_lo, p_hi, k_ref, k_lo, k_hi, base, leak, *rest):
    out = rest[-1]
    z = plane_of(pl.program_id(0))
    top = p_ref.shape[0] - 1
    p = p_ref[z]
    k = k_ref[z]
    up = jnp.minimum(z + 1, top)
    down = jnp.maximum(z - 1, 0)
    p_up = jnp.where(z == top, p_hi[0], p_ref[up])
    k_up = jnp.where(z == top, k_hi[0], k_ref[up])
    p_down = jnp.where(z == 0, p_lo[0], p_ref[down])
    k_down = jnp.where(z == 0, k_lo[0], k_ref[down])
    rows, cols = p.shape
    row = jax.lax.broadcasted_iota(jnp.int32, (rows, cols), 0)
    col = jax.lax.broadcasted_iota(jnp.int32, (rows, cols), 1)

    def side(v, axis, step, edge):
        size = v.shape[axis]
        moved = pltpu.roll(v, (size - step) % size, axis)
        return jnp.where(edge, 0.0, moved)

    x_hi = row == rows - 1
    x_lo = row == 0
    y_hi = col == cols - 1
    y_lo = col == 0
    sides = [
        (p_up, k_up),
        (p_down, k_down),
        (side(p, 0, 1, x_hi), side(k, 0, 1, x_hi)),
        (side(p, 0, -1, x_lo), side(k, 0, -1, x_lo)),
        (side(p, 1, 1, y_hi), side(k, 1, 1, y_hi)),
        (side(p, 1, -1, y_lo), side(k, 1, -1, y_lo)),
    ]
    numerator = base[0] + leak[0]
    denominator = jnp.full(p.shape, UPTAKE, jnp.float32)
    for p_side, k_side in sides:
        facing = 0.5 * (k + k_side)
        numerator = numerator + facing * p_side
        denominator = denominator + facing
    out[0] = numerator / denominator


def relax_sweep(p, p_lo, p_hi, p_at, k, k_lo, k_hi, k_at, base, leak, plane_of, count, into=None):
    planes, rows, cols = base.shape
    whole = pl.BlockSpec((planes, rows, cols), lambda z: (0, 0, 0))
    plane = pl.BlockSpec((1, rows, cols), lambda z: (plane_of(z), 0, 0))

    def edge(at):
        return pl.BlockSpec((None, 1, rows, cols), lambda z: (at, 0, 0, 0))

    specs = [whole, edge(p_at), edge(p_at), whole, edge(k_at), edge(k_at), plane, plane]
    operands = [p, p_lo, p_hi, k, k_lo, k_hi, base, leak]
    aliases = {}
    if into is not None:
        specs.append(pl.BlockSpec(memory_space=pl.ANY))
        operands.append(into)
        aliases = {len(operands) - 1: 0}
    return pl.pallas_call(
        functools.partial(_relax_kernel, plane_of),
        grid=(count,),
        in_specs=specs,
        out_specs=plane,
        out_shape=jax.ShapeDtypeStruct(base.shape, jnp.float32),
        input_output_aliases=aliases,
    )(*operands)


def halos(cells):
    count = lax.axis_size(AXES)
    ends = count - 1
    last = cells.shape[1] - 1
    lo = lax.ppermute(cells[:, last:], AXES, [(i, i + 1) for i in range(ends)])
    hi = lax.ppermute(cells[:, :1], AXES, [(i + 1, i) for i in range(ends)])
    return lo, hi


def pad_sides(values):
    return jnp.pad(values, ((0, 0), (1, 1), (1, 1)))


def bf16_round(x):
    return x.astype(jnp.bfloat16).astype(jnp.float32)


def on_device(
    vessel_start,
    drive,
    junction_gain,
    parent,
    inverse_blocks,
    wall_perm,
    outside,
    owner,
    target,
    kernel_id,
    kernels,
    tissue_start,
    conduct,
    base_source,
):
    devices = lax.axis_size(AXES)
    nb = drive.shape[0]
    seg = drive.shape[1]
    lane = jnp.arange(seg, dtype=jnp.int32)[None, :]
    fixed_rhs = jnp.where(lane == 0, 0.0, drive).astype(jnp.bfloat16)
    unit = jnp.broadcast_to((lane == 0).astype(jnp.bfloat16), (nb, seg))
    both = jnp.einsum(
        "bij,cbj->cbi",
        inverse_blocks,
        jnp.stack([fixed_rhs, unit]),
        preferred_element_type=jnp.float32,
    )
    base = both[0]
    first_col = both[1]
    last_row = inverse_blocks[:, -1, :].astype(jnp.float32)
    exit_base = jnp.sum(last_row * fixed_rhs.astype(jnp.float32), axis=1)
    exit_col = last_row[:, 0]
    drive0 = drive[:, 0]
    packed = jnp.stack(
        [
            exit_base,
            exit_col,
            drive0,
            junction_gain,
            vessel_start[:, -1],
            parent.astype(jnp.float32),
        ]
    ).reshape(1, 6 * nb)
    sent = jnp.broadcast_to(packed, (devices, 6 * nb))
    got = lax.all_to_all(sent, AXES, 0, 0, tiled=True)
    owners = jnp.arange(devices, dtype=jnp.int32)[None, :]
    within = jnp.arange(nb, dtype=jnp.int32)[None, :]

    def fetch(index):
        pick = (index // nb)[:, None] == owners
        rows = jnp.dot(
            pick.astype(jnp.float32), got, precision=lax.Precision.HIGHEST
        ).reshape(index.shape[0], 6, nb)
        lanes = ((index % nb)[:, None] == within)[:, None, :]
        return jnp.sum(jnp.where(lanes, rows, 0.0), axis=2).T

    at1 = fetch(parent)
    p2 = jnp.round(at1[5]).astype(jnp.int32)
    at2 = fetch(p2)
    p3 = jnp.round(at2[5]).astype(jnp.int32)
    x0 = fetch(p3)[4]
    exit1 = at2[0] + at2[1] * bf16_round(at2[2] + at2[3] * x0)
    exit2 = at1[0] + at1[1] * bf16_round(at1[2] + at1[3] * exit1)
    r0 = bf16_round(drive0 + junction_gain * exit2)
    pressure = base + first_col * r0[:, None]
    leak = (wall_perm * (pressure - outside)).astype(jnp.bfloat16)
    destination = owner[:, 0]
    same = destination[:, None] == destination[None, :]
    earlier = jnp.arange(nb)[None, :] < jnp.arange(nb)[:, None]
    slot = jnp.sum((same & earlier).astype(jnp.int32), axis=1)
    capacity = 2
    row_of = destination * capacity + slot
    slots = devices * capacity
    onehot = row_of[None, :] == jnp.arange(slots, dtype=jnp.int32)[:, None]
    leak_sent = jnp.dot(
        onehot.astype(jnp.bfloat16), leak, preferred_element_type=jnp.float32
    ).astype(jnp.bfloat16)
    kid_sent = jnp.sum(jnp.where(onehot, kernel_id[None, :], 0), axis=1)
    tgt_sent = jnp.sum(jnp.where(onehot, target[None, :], 0), axis=1)
    cells = jnp.zeros((slots, seg), jnp.float32)
    for k in range(kernels.shape[0]):
        part = jnp.dot(leak_sent, kernels[k], preferred_element_type=jnp.float32)
        cells = jnp.where((kid_sent == k)[:, None], part, cells)
    tgt_row = jnp.pad(
        tgt_sent.astype(jnp.float32).reshape(devices, capacity), ((0, 0), (0, seg - capacity))
    )
    send = jnp.concatenate(
        [cells.reshape(devices, capacity, seg), tgt_row[:, None, :]], axis=1
    )
    recv = lax.all_to_all(
        send.reshape(devices, (capacity + 1) * seg), AXES, 0, 0, tiled=True
    ).reshape(devices, capacity + 1, seg)
    got_rows = recv[:, :capacity, :].reshape(slots, seg)
    got_index = recv[:, capacity, :capacity].reshape(slots).astype(jnp.int32)
    cell_blocks = tissue_start.size // seg
    leakage = jax.ops.segment_sum(got_rows, got_index, num_segments=cell_blocks)
    leak_field = leakage.reshape(base_source.shape)
    lo, hi = halos(jnp.stack([tissue_start, conduct]))
    planes = base_source.shape[0]
    args = (tissue_start, lo, hi, 0, conduct, lo, hi, 1, base_source, leak_field)
    ends = relax_sweep(*args, lambda z: z * (planes - 1), 2)
    first_lo, first_hi = halos(ends[None])
    first = relax_sweep(*args, lambda z: z + 1, planes - 2, into=ends)
    tissue = relax_sweep(
        first, first_lo, first_hi, 0, conduct, lo, hi, 1, base_source, leak_field,
        lambda z: z, planes,
    )
    return (pressure, tissue)


def solution(mesh):
    in_specs = (
        P(AXES, None),
        P(AXES, None),
        P(AXES),
        P(AXES),
        P(AXES, None, None),
        P(AXES, None),
        P(AXES, None),
        P(AXES, None),
        P(AXES),
        P(AXES),
        P(),
        P(AXES, None, None),
        P(AXES, None, None),
        P(AXES, None, None),
    )
    out_specs = (P(AXES, None), P(AXES, None, None))
    return jax.shard_map(
        on_device, mesh=mesh, in_specs=in_specs, out_specs=out_specs, check_vma=False
    )
```
